256 devices in a mesh: req: 8 (over z), exp: 8 (over y, core), hid: 4 (over x).
Axes of the slice: x: 4, y: 4, z: 8, core: 2. Of those that a mesh axis runs over, the one named last changes fastest.
Arguments:
- layer_input_rows: bfloat16 [16384, 1536], P(('req', 'exp')), may hold values from -6 to 6
- attention_norm_gain: float32 [1536], replicated
- query_weight: bfloat16 [1536, 1536], P(None, 'hid'), may hold values from -1 to 1
- key_weight: bfloat16 [1536, 512], P(None, 'hid'), may hold values from -1 to 1
- value_weight: bfloat16 [1536, 512], P(None, 'hid'), may hold values from -0.15625 to 0.15625
- attention_output_weight: bfloat16 [1536, 1536], P('hid'), may hold values from -0.15625 to 0.15625
- query_down_factor: bfloat16 [64, 1536, 16], P(('req', 'exp')), may hold values from -0.15625 to 0.15625
- query_up_factor: bfloat16 [64, 16, 1536], P(('req', 'exp')), may hold values from -1.5 to 1.5
- value_down_factor: bfloat16 [64, 1536, 16], P(('req', 'exp')), may hold values from -0.15625 to 0.15625
- value_up_factor: bfloat16 [64, 16, 512], P(('req', 'exp')), may hold values from -1.5 to 1.5
- lengths: int32 [8, 4], P('req'), may hold values from 1 to 1024, 2048 in all within a row
- request_adapter: int32 [8, 4], replicated, may hold values from 0 to 63
- adapter_home_row: int32 [64], replicated, may hold values from 0 to 63, each once
- expert_norm_gain: float32 [1536], replicated, may hold values from 0.4 to 1.6
- routes: int32 [16384, 8], P(('req', 'exp', 'hid')), may hold values from 0 to 39, all different within a row; in each aligned block of 64 rows (0 to 63, 64 to 127, ...) at most 16 rows name the same one
- router_expert_weight: float32 [16384, 8], P(('req', 'exp', 'hid')), may hold values from 0.1 to 0.5
- expert_gate_weight: bfloat16 [40, 1536, 512], P('exp', None, 'hid'), may hold values from -0.15625 to 0.15625
- expert_up_weight: bfloat16 [40, 1536, 512], P('exp', None, 'hid'), may hold values from -0.15625 to 0.15625
- expert_down_weight: bfloat16 [40, 512, 1536], P('exp', 'hid'), may hold values from -0.25 to 0.25
Outputs:
- attn_out: bfloat16 [16384, 1536], P(('req', 'exp', 'hid'))
- expert_out: bfloat16 [16384, 1536], P(('req', 'exp', 'hid'))
The draws below stay inside these ranges and needn't reach their ends.
Inputs may be any that keep to these rules, and one draw needn't show every extreme that they name: `lengths`: each row sums to 2048; its largest entry is exactly 1024. `adapter_home_row`: each adapter row appears once. `routes`: A row names 8 different experts. In the rows of one device (64 consecutive rows, aligned) no expert is named more than 16 times, a bound that some block reaches in some of them.
All inputs are finite; a program needn't handle non-finite values.
Results may differ from the reference program's by a relative error of at most 0.029.
The reference program's roundings to bfloat16 on the way count: a program that leaves them out, or rounds other values in their place, can miss the bound.
Values may be sent and summed in bfloat16 or wider, within the bound.
No kernel may reach another device: no remote copies, remote signals or barrier semaphores. Data moves between devices by JAX's collectives and lax.ppermute only.
A program may use at most 128 MiB of HBM per device.

```python
import math
import jax
import jax.numpy as jnp
import numpy as np
from jax import lax

MODEL_WIDTH = 1536
QUERY_HEADS = 24
KEY_VALUE_HEADS = 8
HEAD_WIDTH = 64
EXPERTS = 40
FF = 512
TOP = 8
ADAPTER_RANK = 16
ADAPTER_COUNT = 64
REQS = 4
TOK_DEV = 64
TOK_REQ = 2048
GROUPS = 8
TOKENS = 16384
CAP = 16
LONGEST = 1024
N_HID = 4


def query_key_draw(key):
    query_base = jnp.clip(jax.random.normal(jax.random.fold_in(key, 11), (MODEL_WIDTH, QUERY_HEADS * HEAD_WIDTH), jnp.float32), -6.0, 6.0) * MODEL_WIDTH ** (-0.5)
    noise_part = jnp.clip(jax.random.normal(jax.random.fold_in(key, 12), (MODEL_WIDTH, KEY_VALUE_HEADS * HEAD_WIDTH), jnp.float32), -6.0, 6.0) * MODEL_WIDTH ** (-0.5)
    return (query_base, noise_part)


def draw_query_weight(key, part):
    query_base, noise_part = query_key_draw(key)
    return jnp.clip(query_base, -1.0, 1.0).astype(jnp.bfloat16)


def draw_key_weight(key, part):
    query_base, noise_part = query_key_draw(key)
    return jnp.clip(noise_part, -1.0, 1.0).astype(jnp.bfloat16)


def draw_attention_norm_gain(key, part):
    return 1.0 + 0.1 * jnp.clip(jax.random.normal(jax.random.fold_in(key, 22), (MODEL_WIDTH,), jnp.float32), -4.0, 4.0)


def touch_ends(values, rng, least, top_value):
    place = [jax.random.randint(jax.random.fold_in(rng, axis), (), 0, length) for axis, length in enumerate(values.shape)]
    longest = values.shape.index(max(values.shape))
    next_to = place[:longest] + [(place[longest] + 1) % values.shape[longest]] + place[longest + 1:]
    return values.at[tuple(place)].set(least).at[tuple(next_to)].set(top_value)


def block_levels(rng, dims, cuts, smallest, top_value):
    factor_of = 1.0
    for axis_at, shards_of in cuts:
        draws = jax.random.uniform(jax.random.fold_in(jax.random.fold_in(rng, 6), axis_at), (shards_of,), jnp.float32, smallest / len(cuts), top_value / len(cuts))
        factor_of = factor_of * jnp.repeat(jnp.exp(draws), dims[axis_at] // shards_of).reshape((-1,) + (1,) * (len(dims) - 1 - axis_at))
    return factor_of


def split_up(amount, total, most, lean):
    loads = [(1 << 20) // math.isqrt(grade ** lean) + 1 for grade in range(2, amount + 1)]
    surplus, given = total - most - (amount - 1), [1] * (amount - 1)
    while surplus > 0:
        free = [i for i in range(amount - 1) if given[i] < most]
        pool, budget = sum([loads[i] for i in free]), surplus
        for i in free:
            addition = min(most - given[i], max(1, budget * loads[i] // pool), surplus)
            given[i] = given[i] + addition
            surplus = surplus - addition
    return np.array([most] + given)


def ragged_sizes(own_key, amount, total, most, skew):
    if amount == 2:
        one = jax.random.randint(own_key, (), max(1, total - most), min(most, total - 1) + 1)
        return jnp.stack([one, total - one])
    sizes = jnp.asarray(split_up(amount, total, most, skew), jnp.int32)
    twos = (amount - 1) // 2
    source_of, receiver = sizes[1:1 + 2 * twos:2], sizes[2:2 + 2 * twos:2]
    slack = jnp.minimum(source_of - 1, most - receiver)
    moved = jax.random.randint(jax.random.fold_in(own_key, 1), (twos,), 0, 1 << 20) % (slack + 1)
    sizes = sizes.at[1:1 + 2 * twos:2].set(source_of - moved).at[2:2 + 2 * twos:2].set(receiver + moved)
    return sizes[jax.random.permutation(jax.random.fold_in(own_key, 2), amount)]


def routed_block(key, own, number, rows, count, top, most, skew):
    ranking = jax.random.permutation(key, count)
    crowded, usual = portions_of(count, rows * top, most, skew, True), portions_of(count, rows * top, most, skew, False)
    places = jnp.arange(count)

    def named(sizes, rotation):
        used = int((sizes > 0).sum())
        fixed = max(1, used // 4)
        moved = fixed + (places - fixed + rotation * (used - fixed)) % max(1, count - fixed)
        return jnp.zeros((count,), jnp.int32).at[ranking[jnp.where(places < fixed, places, moved)]].set(jnp.asarray(sizes, jnp.int32))

    sizes = jnp.where(number % 4 == 0, named(crowded, number // 4), named(usual, number - number // 4 - 1))
    mixed = jax.random.permutation(jax.random.fold_in(own, 3), count)
    source_of, taker = mixed[0:count // 2 * 2:2], mixed[1:count // 2 * 2:2]
    margin = jnp.minimum(sizes[source_of] - 1, most - sizes[taker]) // 2
    margin = jnp.where((source_of == ranking[0]) | (taker == ranking[0]) | (sizes[taker] == 0), 0, jnp.maximum(margin, 0))
    moved = jax.random.randint(jax.random.fold_in(own, 4), (count // 2,), 0, 1 << 20) % (margin + 1)
    sizes = sizes.at[source_of].add(-moved).at[taker].add(moved)
    labels = jnp.searchsorted(jnp.cumsum(sizes), jnp.arange(rows * top), side="right").astype(jnp.int32)
    table = labels.reshape(top, rows).T
    table = table[jax.random.permutation(jax.random.fold_in(own, 1), rows)]
    rotation = jax.random.randint(jax.random.fold_in(own, 2), (rows, 1), 0, top)
    return jnp.take_along_axis(table, (jnp.arange(top)[None, :] + rotation) % top, axis=1)


def portions_of(number_of, total, bound, lean, full):
    loads = [(1 << 20) // math.isqrt(standing ** lean) + 1 for standing in range(1, number_of + 1)]
    largest = bound if full else min(bound, max(-(-total // number_of), total * loads[0] // sum(loads)))
    least = 1 if total - largest >= number_of - 1 else 0
    given, surplus = [largest] + [least] * (number_of - 1), total - largest - least * (number_of - 1)
    while surplus > 0:
        candidates = [i for i in range(1, number_of) if given[i] < largest] or [i for i in range(1, number_of) if given[i] < bound]
        pool, remaining = sum([loads[i] for i in candidates]), surplus
        for i in candidates:
            addition = min(bound - given[i], max(1, remaining * loads[i] // pool), surplus)
            given[i] = given[i] + addition
            surplus = surplus - addition
    return np.array(given)


def normal_values(key, shape, scale, limit, pieces=(), kind=jnp.bfloat16):
    factor_of = block_levels(key, shape, pieces, -0.22, 0.18) if pieces else 1.0
    values = jax.random.normal(key, shape, jnp.float32) * scale * factor_of
    return jnp.minimum(jnp.maximum(values, -limit), limit).astype(kind)


def setup_inputs(seed: int = 0) -> dict:
    key_of = jax.random.split(jax.random.key(seed), 20)
    layer_input_rows = normal_values(key_of[0], (TOKENS, MODEL_WIDTH), 1.0, 6.0, ((0, 64),))
    attention_norm_gain = draw_attention_norm_gain(jax.random.fold_in(key_of[19], 71), 0)
    query_weight = draw_query_weight(jax.random.fold_in(key_of[19], 71), 0)
    key_weight = draw_key_weight(jax.random.fold_in(key_of[19], 71), 0)
    value_weight = normal_values(key_of[4], (MODEL_WIDTH, KEY_VALUE_HEADS * HEAD_WIDTH), MODEL_WIDTH ** -0.5, 0.15625, ((1, 4),))
    attention_output_weight = normal_values(key_of[5], (QUERY_HEADS * HEAD_WIDTH, MODEL_WIDTH), (QUERY_HEADS * HEAD_WIDTH) ** -0.5, 0.15625, ((0, 4),))
    query_down_factor = normal_values(key_of[6], (ADAPTER_COUNT, MODEL_WIDTH, ADAPTER_RANK), MODEL_WIDTH ** -0.5, 0.15625, ((0, 64),))
    query_up_factor = normal_values(key_of[7], (ADAPTER_COUNT, ADAPTER_RANK, QUERY_HEADS * HEAD_WIDTH), ADAPTER_RANK ** -0.5, 1.5, ((0, 64),))
    value_down_factor = normal_values(key_of[8], (ADAPTER_COUNT, MODEL_WIDTH, ADAPTER_RANK), MODEL_WIDTH ** -0.5, 0.15625, ((0, 64),))
    value_up_factor = normal_values(key_of[9], (ADAPTER_COUNT, ADAPTER_RANK, KEY_VALUE_HEADS * HEAD_WIDTH), ADAPTER_RANK ** -0.5, 1.5, ((0, 64),))
    lengths = jax.vmap(lambda own: ragged_sizes(own, REQS, TOK_REQ, LONGEST, 2))(jax.random.split(key_of[10], GROUPS)).reshape((GROUPS, REQS)).astype(jnp.int32)
    request_adapter = touch_ends(jax.random.randint(key_of[11], (GROUPS, REQS), 0, ADAPTER_COUNT), jax.random.fold_in(key_of[11], 1), 0, ADAPTER_COUNT - 1).astype(jnp.int32)
    adapter_home_row = jax.random.permutation(key_of[12], ADAPTER_COUNT).astype(jnp.int32)
    expert_norm_gain = jnp.clip(1.0 + 0.12 * jax.random.normal(key_of[13], (MODEL_WIDTH,), jnp.float32), 0.4, 1.6)
    routes_keys = jax.random.split(jax.random.fold_in(key_of[14], 1), TOKENS // TOK_DEV)
    routes_turns = jax.random.permutation(jax.random.fold_in(key_of[14], 3), TOKENS // TOK_DEV)
    routes = jax.vmap(lambda own, number: routed_block(jax.random.fold_in(key_of[14], 2), own, number, TOK_DEV, EXPERTS, TOP, CAP, 1))(routes_keys, routes_turns).reshape((TOKENS, TOP))
    router_expert_weight = jnp.clip(0.1 + 0.4 * jax.random.uniform(key_of[15], (TOKENS, TOP), jnp.float32) ** block_levels(key_of[15], (TOKENS, TOP), ((0, 256),), -0.2, 0.2), 0.1, 0.5)
    expert_gate_weight = normal_values(key_of[16], (EXPERTS, MODEL_WIDTH, FF), MODEL_WIDTH ** -0.5, 0.15625, ((0, 8), (2, 4)))
    expert_up_weight = normal_values(key_of[17], (EXPERTS, MODEL_WIDTH, FF), MODEL_WIDTH ** -0.5, 0.15625, ((0, 8), (2, 4)))
    expert_down_weight = normal_values(key_of[18], (EXPERTS, FF, MODEL_WIDTH), FF ** -0.5, 0.25, ((0, 8), (1, 4)))
    return dict(layer_input_rows=layer_input_rows, attention_norm_gain=attention_norm_gain, query_weight=query_weight, key_weight=key_weight, value_weight=value_weight, attention_output_weight=attention_output_weight, query_down_factor=query_down_factor, query_up_factor=query_up_factor, value_down_factor=value_down_factor, value_up_factor=value_up_factor, lengths=lengths, request_adapter=request_adapter, adapter_home_row=adapter_home_row, expert_norm_gain=expert_norm_gain, routes=routes, router_expert_weight=router_expert_weight, expert_gate_weight=expert_gate_weight, expert_up_weight=expert_up_weight, expert_down_weight=expert_down_weight)


scale_attn = 0.015625
residual_mult = 0.22
norm_eps = 1e-06
rope_base = 10000.0
neg_large = -1e+30

def rms_norm(values, norm_gain):
    widened = values.astype(jnp.float32)
    mean_sq = lax.optimization_barrier(jnp.mean(widened * widened, axis=-1, keepdims=True))
    return (widened * lax.rsqrt(mean_sq + norm_eps) * norm_gain).astype(jnp.bfloat16)

def rotary(heads_in, position):
    half_size = heads_in.shape[-1] // 2
    frequency = rope_base ** (-2.0 * jnp.arange(half_size, dtype=jnp.float32) / heads_in.shape[-1])
    angles = position.astype(jnp.float32)[:, None] * frequency[None, :]
    cosine = jnp.cos(angles)[:, None, :]
    sine_part = jnp.sin(angles)[:, None, :]
    first_half = heads_in[..., :half_size]
    second_half = heads_in[..., half_size:]
    return jnp.concatenate([first_half * cosine - second_half * sine_part, second_half * cosine + first_half * sine_part], axis=-1)

def locate(row_ids, group_len):
    request_end = jnp.cumsum(group_len).astype(jnp.int32)
    request_start = (request_end - group_len).astype(jnp.int32)
    request = lax.optimization_barrier(jnp.sum((row_ids[:, None] >= request_end[None, :]).astype(jnp.int32), axis=1)).astype(jnp.int32)
    member = request[:, None] == jnp.arange(group_len.shape[0], dtype=jnp.int32)[None, :]
    position = (row_ids - lax.optimization_barrier(jnp.sum(jnp.where(member, request_start[None, :], 0), axis=1))).astype(jnp.int32)
    return (request, member, position)

def reference(layer_input_rows, attention_norm_gain, query_weight, key_weight, value_weight, attention_output_weight, query_down_factor, query_up_factor, value_down_factor, value_up_factor, lengths, request_adapter, adapter_home_row, expert_norm_gain, routes, router_expert_weight, expert_gate_weight, expert_up_weight, expert_down_weight):
    group_share = QUERY_HEADS // KEY_VALUE_HEADS

    def group_attention(group_id):
        group_x = lax.dynamic_slice_in_dim(layer_input_rows, group_id * TOK_REQ, TOK_REQ, 0)
        group_len = lengths[group_id]
        row_ids = jnp.arange(TOK_REQ, dtype=jnp.int32)
        request, member, position = locate(row_ids, group_len)
        adapter_bank_rows = adapter_home_row[request_adapter[group_id]]
        normed_rows = rms_norm(group_x, attention_norm_gain)

        def low_rank_term(a_sel, b_sel):
            inner_terms = jnp.einsum('td,jdr->tjr', normed_rows.astype(jnp.float32), a_sel.astype(jnp.float32))
            inner_terms = jnp.where(member[:, :, None], inner_terms, 0.0).reshape(TOK_REQ, REQS * ADAPTER_RANK).astype(jnp.bfloat16)
            right_factor = b_sel.reshape(REQS * ADAPTER_RANK, b_sel.shape[2])
            return jnp.dot(inner_terms, right_factor, preferred_element_type=jnp.float32)
        query_matrix = jnp.dot(normed_rows, query_weight, preferred_element_type=jnp.float32) + low_rank_term(query_down_factor[adapter_bank_rows], query_up_factor[adapter_bank_rows])
        query_matrix = rotary(query_matrix.reshape(TOK_REQ, QUERY_HEADS, HEAD_WIDTH), position).astype(jnp.bfloat16)
        keys_all = jnp.dot(normed_rows, key_weight, preferred_element_type=jnp.float32)
        keys_all = rotary(keys_all.reshape(TOK_REQ, KEY_VALUE_HEADS, HEAD_WIDTH), position).astype(jnp.bfloat16)
        value_rows_all = jnp.dot(normed_rows, value_weight, preferred_element_type=jnp.float32) + low_rank_term(value_down_factor[adapter_bank_rows], value_up_factor[adapter_bank_rows])
        value_rows_all = value_rows_all.astype(jnp.bfloat16).reshape(TOK_REQ, KEY_VALUE_HEADS, HEAD_WIDTH)
        allowed = (request[:, None] == request[None, :]) & (row_ids[None, :] <= row_ids[:, None])

        def one_head(head_id):
            query_head = lax.dynamic_index_in_dim(query_matrix, head_id, 1, keepdims=False)
            key_head = lax.dynamic_index_in_dim(keys_all, head_id // group_share, 1, keepdims=False)
            value_head = lax.dynamic_index_in_dim(value_rows_all, head_id // group_share, 1, keepdims=False)
            scores = jnp.dot(query_head, key_head.T, preferred_element_type=jnp.float32) * scale_attn
            scores = jnp.where(allowed, scores, neg_large)
            row_max = lax.optimization_barrier(jnp.max(scores, axis=-1, keepdims=True))
            weights = jnp.where(allowed, jnp.exp(scores - row_max), 0.0)
            row_sum = lax.optimization_barrier(jnp.sum(weights, axis=-1, keepdims=True))
            mixed_values = jnp.dot(weights.astype(jnp.bfloat16), value_head, preferred_element_type=jnp.float32)
            return (mixed_values / row_sum).astype(jnp.bfloat16)
        heads_out = lax.map(one_head, jnp.arange(QUERY_HEADS, dtype=jnp.int32))
        attended = jnp.transpose(heads_out, (1, 0, 2)).reshape(TOK_REQ, QUERY_HEADS * HEAD_WIDTH)
        return jnp.dot(attended, attention_output_weight, preferred_element_type=jnp.float32).astype(jnp.bfloat16)
    attn_out = lax.map(group_attention, jnp.arange(GROUPS, dtype=jnp.int32)).reshape(TOKENS, MODEL_WIDTH)
    mixed_rows = layer_input_rows.astype(jnp.float32) + residual_mult * attn_out.astype(jnp.float32)
    normed_moe = rms_norm(mixed_rows, expert_norm_gain)
    most_rows = TOKENS // TOK_DEV * CAP
    slice_size = FF // N_HID

    def one_expert(total_in, expert_id):
        matched = routes == expert_id
        route_gain = lax.optimization_barrier(jnp.sum(jnp.where(matched, router_expert_weight, 0.0), axis=1))
        chosen = jnp.any(matched, axis=1)
        take_ids = jnp.nonzero(chosen, size=most_rows, fill_value=TOKENS)[0].astype(jnp.int32)
        rows_in = jnp.take(normed_moe, take_ids, axis=0, mode='fill', fill_value=0)
        gate_act = jnp.dot(rows_in, expert_gate_weight[expert_id], preferred_element_type=jnp.float32)
        upper = jnp.dot(rows_in, expert_up_weight[expert_id], preferred_element_type=jnp.float32)
        hidden = (jax.nn.silu(gate_act) * upper).astype(jnp.bfloat16)
        hidden_slices = hidden.reshape(most_rows, N_HID, slice_size).astype(jnp.float32)
        down_slices = expert_down_weight[expert_id].reshape(N_HID, slice_size, MODEL_WIDTH).astype(jnp.float32)
        partials = jnp.einsum('rcf,cfd->rcd', hidden_slices, down_slices).astype(jnp.bfloat16)
        result = lax.optimization_barrier(jnp.sum(partials.astype(jnp.float32), axis=1)).astype(jnp.bfloat16)
        gained = jnp.take(route_gain, take_ids, mode='fill', fill_value=0.0)[:, None] * result.astype(jnp.float32)
        return (total_in.at[take_ids].add(gained, mode='drop'), None)
    total_out, unused = lax.scan(one_expert, jnp.zeros((TOKENS, MODEL_WIDTH), jnp.float32), jnp.arange(EXPERTS, dtype=jnp.int32))
    return (attn_out, total_out.astype(jnp.bfloat16))
```

```python
import jax
import jax.numpy as jnp
from jax import lax
from jax.sharding import PartitionSpec as P

HEAD_WIDTH = 64


scale_attn = 0.015625
residual_mult = 0.22
norm_eps = 1e-06
rope_base = 10000.0
neg_large = -1e30


def rms_norm(values, norm_gain):
    widened = values.astype(jnp.float32)
    mean_sq = jnp.mean(widened * widened, axis=-1, keepdims=True)
    return (widened * lax.rsqrt(mean_sq + norm_eps) * norm_gain).astype(jnp.bfloat16)


def rotary(heads_in, position):
    half_size = heads_in.shape[-1] // 2
    frequency = rope_base ** (-2.0 * jnp.arange(half_size, dtype=jnp.float32) / heads_in.shape[-1])
    angles = position.astype(jnp.float32)[:, None] * frequency[None, :]
    cosine = jnp.cos(angles)[:, None, :]
    sine_part = jnp.sin(angles)[:, None, :]
    first_half = heads_in[..., :half_size]
    second_half = heads_in[..., half_size:]
    return jnp.concatenate(
        [
            first_half * cosine - second_half * sine_part,
            second_half * cosine + first_half * sine_part,
        ],
        axis=-1,
    )


def request_of(row_ids, group_len):
    request_end = jnp.cumsum(group_len)
    return jnp.sum((row_ids[:, None] >= request_end[None, :]).astype(jnp.int32), axis=1)


def locate(row_ids, group_len):
    request_end = jnp.cumsum(group_len)
    request_start = request_end - group_len
    request = request_of(row_ids, group_len)
    member = request[:, None] == jnp.arange(group_len.shape[0], dtype=jnp.int32)[None, :]
    position = row_ids - jnp.sum(jnp.where(member, request_start[None, :], 0), axis=1)
    return (request, member, position)


def expert_rows(rows_in, expert_gate_weight, expert_up_weight, expert_down_weight):
    gate_act = jnp.einsum(
        "red,edf->ref", rows_in, expert_gate_weight, preferred_element_type=jnp.float32
    )
    upper = jnp.einsum(
        "red,edf->ref", rows_in, expert_up_weight, preferred_element_type=jnp.float32
    )
    hidden = (jax.nn.silu(gate_act) * upper).astype(jnp.bfloat16)
    return jnp.einsum(
        "ref,efd->red", hidden, expert_down_weight, preferred_element_type=jnp.float32
    )


def per_device(
    layer_input_rows,
    attention_norm_gain,
    query_weight,
    key_weight,
    value_weight,
    attention_output_weight,
    query_down_factor,
    query_up_factor,
    value_down_factor,
    value_up_factor,
    lengths,
    request_adapter,
    adapter_home_row,
    expert_norm_gain,
    routes,
    router_expert_weight,
    expert_gate_weight,
    expert_up_weight,
    expert_down_weight,
):
    exp_count = lax.axis_size("exp")
    hid_count = lax.axis_size("hid")
    exp_index = lax.axis_index("exp")
    hid_index = lax.axis_index("hid")
    req_index = lax.axis_index("req")
    query_rows = layer_input_rows.shape[0]
    width = layer_input_rows.shape[1]
    kv_local = key_weight.shape[1] // HEAD_WIDTH
    q_local = query_weight.shape[1] // HEAD_WIDTH
    group_share = q_local // kv_local
    adapter_rank_size = query_down_factor.shape[2]
    requests = lengths.shape[1]
    group_len = lengths[0]
    row_ids = exp_index * query_rows + jnp.arange(query_rows, dtype=jnp.int32)
    request, member, position = locate(row_ids, group_len)
    wanted = lax.dynamic_index_in_dim(request_adapter, req_index, 0, keepdims=False)
    slot_ids = jnp.arange(adapter_home_row.shape[0], dtype=jnp.int32)
    home_of = jnp.sum(
        jnp.where(wanted[:, None] == slot_ids[None, :], adapter_home_row[None, :], 0), axis=1
    )
    query_cols = q_local * HEAD_WIDTH
    kv_cols = kv_local * HEAD_WIDTH
    bank_local = query_down_factor.shape[0]
    up_q = lax.dynamic_slice_in_dim(query_up_factor, hid_index * query_cols, query_cols, 2)
    up_v = lax.dynamic_slice_in_dim(value_up_factor, hid_index * kv_cols, kv_cols, 2)
    parts_in = (query_down_factor, up_q, value_down_factor, up_v)
    part_shapes = [p.shape[1:] for p in parts_in]
    part_sizes = [p.shape[1] * p.shape[2] for p in parts_in]
    bank = jnp.concatenate([p.reshape(bank_local, -1) for p in parts_in], axis=1)
    along_req = lax.all_gather(bank, "req", axis=0, tiled=True)
    home_dev = home_of // bank_local
    home_pick = (home_dev // exp_count) * bank_local + home_of % bank_local
    mine = (home_dev % exp_count) == exp_index
    rows_pick = jnp.take(along_req, home_pick, axis=0)
    rows_pick = jnp.where(mine[:, None], rows_pick, jnp.zeros_like(rows_pick))
    rows_pick = lax.psum(rows_pick, "exp")
    chosen = []
    start = 0
    for shape_in, size_in in zip(part_shapes, part_sizes):
        chosen.append(rows_pick[:, start:start + size_in].reshape((requests,) + shape_in))
        start += size_in
    qa_sel, qb_sel, va_sel, vb_sel = chosen
    normed_rows = rms_norm(layer_input_rows, attention_norm_gain)

    def low_rank_term(a_sel, b_sel, width_cols, offset):
        inner_terms = jnp.einsum(
            "td,jdr->tjr", normed_rows, a_sel, preferred_element_type=jnp.float32
        )
        inner_terms = (
            jnp.where(member[:, :, None], inner_terms, 0.0)
            .reshape(query_rows, requests * adapter_rank_size)
            .astype(jnp.bfloat16)
        )
        right_factor = b_sel.reshape(requests * adapter_rank_size, width_cols)
        return jnp.dot(inner_terms, right_factor, preferred_element_type=jnp.float32)

    query_matrix = jnp.dot(
        normed_rows, query_weight, preferred_element_type=jnp.float32
    ) + low_rank_term(qa_sel, qb_sel, query_cols, hid_index * query_cols)
    query_matrix = rotary(query_matrix.reshape(query_rows, q_local, HEAD_WIDTH), position).astype(
        jnp.bfloat16
    )
    query_matrix = query_matrix.reshape(query_rows, kv_local, group_share, HEAD_WIDTH)
    keys_own = jnp.dot(normed_rows, key_weight, preferred_element_type=jnp.float32)
    keys_own = (
        rotary(keys_own.reshape(query_rows, kv_local, HEAD_WIDTH), position)
        .astype(jnp.bfloat16)
        .reshape(query_rows, kv_cols)
    )
    values_own = jnp.dot(
        normed_rows, value_weight, preferred_element_type=jnp.float32
    ) + low_rank_term(va_sel, vb_sel, kv_cols, hid_index * kv_cols)
    values_own = values_own.astype(jnp.bfloat16)
    running_max = jnp.full((kv_local, group_share, query_rows), neg_large, jnp.float32)
    key_piece = lax.all_gather(keys_own, "exp", axis=0, tiled=True)
    value_piece = lax.all_gather(values_own, "exp", axis=0, tiled=True)
    piece_len = key_piece.shape[0]
    key_ids = jnp.arange(piece_len, dtype=jnp.int32)
    key_request = request_of(key_ids, group_len)
    allowed = (request[:, None] == key_request[None, :]) & (key_ids[None, :] <= row_ids[:, None])
    key_heads = key_piece.reshape(piece_len, kv_local, HEAD_WIDTH)
    value_heads = value_piece.reshape(piece_len, kv_local, HEAD_WIDTH)
    scores = (
        jnp.einsum("qkgh,nkh->kgqn", query_matrix, key_heads, preferred_element_type=jnp.float32)
        * scale_attn
    )
    scores = jnp.where(allowed[None, None], scores, neg_large)
    new_max = jnp.maximum(running_max, jnp.max(scores, axis=-1))
    weights = jnp.where(allowed[None, None], jnp.exp(scores - new_max[..., None]), 0.0)
    running_sum = jnp.sum(weights, axis=-1)
    running_out = jnp.einsum(
        "kgqn,nkh->kgqh",
        weights.astype(jnp.bfloat16),
        value_heads,
        preferred_element_type=jnp.float32,
    )
    running_max, running_sum, running_out = (new_max, running_sum, running_out)
    attended = (running_out / running_sum[..., None]).astype(jnp.bfloat16)
    attended = jnp.transpose(attended, (2, 0, 1, 3)).reshape(query_rows, query_cols)
    tok_rows = query_rows // hid_count
    attn_out = lax.psum_scatter(
        jnp.dot(attended, attention_output_weight, preferred_element_type=jnp.float32).astype(
            jnp.bfloat16
        ),
        "hid",
        scatter_dimension=0,
        tiled=True,
    )
    own_rows = lax.dynamic_slice_in_dim(layer_input_rows, hid_index * tok_rows, tok_rows, 0)
    mixed_rows = own_rows.astype(jnp.float32) + residual_mult * attn_out.astype(jnp.float32)
    normed_moe = rms_norm(mixed_rows, expert_norm_gain)
    local_exp = expert_gate_weight.shape[0]
    expert_count = local_exp * exp_count
    top_count = routes.shape[1]
    capacity = max(2, tok_rows // 4)
    flat_route = routes.reshape(tok_rows * top_count)
    route_hits = (flat_route[:, None] == jnp.arange(expert_count, dtype=jnp.int32)[None, :]).astype(
        jnp.int32
    )
    earlier = jnp.cumsum(route_hits, axis=0) - route_hits
    slot_pos = jnp.sum(earlier * route_hits, axis=1)
    slots = slot_pos * expert_count + flat_route
    slot_table = jnp.arange(capacity * expert_count, dtype=jnp.int32)
    placed = jnp.any(
        slot_table[:, None, None] == slots.reshape(tok_rows, top_count)[None], axis=2
    ).astype(jnp.bfloat16)
    outgoing = jnp.dot(placed, normed_moe, preferred_element_type=jnp.float32).astype(jnp.bfloat16)
    outgoing = outgoing.reshape(capacity, expert_count, width)
    copies = jnp.broadcast_to(
        outgoing.reshape(capacity, exp_count, 1, local_exp, width),
        (capacity, exp_count, hid_count, local_exp, width),
    )
    copies = copies.reshape(capacity, exp_count * hid_count * local_exp, width)
    arrived = lax.all_to_all(copies, ("exp", "hid"), split_axis=1, concat_axis=0, tiled=True)
    partials = expert_rows(
        arrived, expert_gate_weight, expert_up_weight, expert_down_weight
    ).astype(jnp.bfloat16)
    returned = lax.all_to_all(partials, ("exp", "hid"), split_axis=0, concat_axis=1, tiled=True)
    returned = returned.reshape(capacity, exp_count, hid_count, local_exp, width)
    results = jnp.sum(returned.astype(jnp.float32), axis=2).astype(jnp.bfloat16)
    results = results.reshape(capacity * expert_count, width)
    picked = jnp.take(results, slots, axis=0).reshape(tok_rows, top_count, width)
    expert_out = jnp.sum(
        router_expert_weight[:, :, None] * picked.astype(jnp.float32), axis=1
    ).astype(jnp.bfloat16)
    return (attn_out, expert_out)


def solution(mesh):
    in_specs = (
        P(("req", "exp"), None),
        P(),
        P(None, "hid"),
        P(None, "hid"),
        P(None, "hid"),
        P("hid", None),
        P(("req", "exp"), None, None),
        P(("req", "exp"), None, None),
        P(("req", "exp"), None, None),
        P(("req", "exp"), None, None),
        P("req", None),
        P(),
        P(),
        P(),
        P(("req", "exp", "hid"), None),
        P(("req", "exp", "hid"), None),
        P("exp", None, "hid"),
        P("exp", None, "hid"),
        P("exp", "hid", None),
    )
    out_specs = (P(("req", "exp", "hid"), None), P(("req", "exp", "hid"), None))
    return jax.shard_map(
        per_device, mesh=mesh, in_specs=in_specs, out_specs=out_specs, check_vma=False
    )
```

```python
import jax
import jax.numpy as jnp
from jax import lax
from jax.sharding import PartitionSpec as P

HEAD_WIDTH = 64


scale_attn = 0.015625
residual_mult = 0.22
norm_eps = 1e-06
rope_base = 10000.0
neg_large = -1e30


def rms_norm(values, norm_gain):
    widened = values.astype(jnp.float32)
    mean_sq = jnp.mean(widened * widened, axis=-1, keepdims=True)
    return (widened * lax.rsqrt(mean_sq + norm_eps) * norm_gain).astype(jnp.bfloat16)


def rotary(heads_in, position):
    half_size = heads_in.shape[-1] // 2
    frequency = rope_base ** (-2.0 * jnp.arange(half_size, dtype=jnp.float32) / heads_in.shape[-1])
    angles = position.astype(jnp.float32)[:, None] * frequency[None, :]
    cosine = jnp.cos(angles)[:, None, :]
    sine_part = jnp.sin(angles)[:, None, :]
    first_half = heads_in[..., :half_size]
    second_half = heads_in[..., half_size:]
    return jnp.concatenate(
        [
            first_half * cosine - second_half * sine_part,
            second_half * cosine + first_half * sine_part,
        ],
        axis=-1,
    )


def request_of(row_ids, group_len):
    request_end = jnp.cumsum(group_len)
    return jnp.sum((row_ids[:, None] >= request_end[None, :]).astype(jnp.int32), axis=1)


def locate(row_ids, group_len):
    request_end = jnp.cumsum(group_len)
    request_start = request_end - group_len
    request = request_of(row_ids, group_len)
    member = request[:, None] == jnp.arange(group_len.shape[0], dtype=jnp.int32)[None, :]
    position = row_ids - jnp.sum(jnp.where(member, request_start[None, :], 0), axis=1)
    return (request, member, position)


def expert_rows(rows_in, expert_gate_weight, expert_up_weight, expert_down_weight):
    gate_act = jnp.einsum(
        "red,edf->ref", rows_in, expert_gate_weight, preferred_element_type=jnp.float32
    )
    upper = jnp.einsum(
        "red,edf->ref", rows_in, expert_up_weight, preferred_element_type=jnp.float32
    )
    hidden = (jax.nn.silu(gate_act) * upper).astype(jnp.bfloat16)
    return jnp.einsum(
        "ref,efd->red", hidden, expert_down_weight, preferred_element_type=jnp.float32
    )


def per_device(
    layer_input_rows,
    attention_norm_gain,
    query_weight,
    key_weight,
    value_weight,
    attention_output_weight,
    query_down_factor,
    query_up_factor,
    value_down_factor,
    value_up_factor,
    lengths,
    request_adapter,
    adapter_home_row,
    expert_norm_gain,
    routes,
    router_expert_weight,
    expert_gate_weight,
    expert_up_weight,
    expert_down_weight,
):
    exp_count = lax.axis_size("exp")
    hid_count = lax.axis_size("hid")
    exp_index = lax.axis_index("exp")
    hid_index = lax.axis_index("hid")
    req_index = lax.axis_index("req")
    query_rows = layer_input_rows.shape[0]
    width = layer_input_rows.shape[1]
    kv_local = key_weight.shape[1] // HEAD_WIDTH
    q_local = query_weight.shape[1] // HEAD_WIDTH
    group_share = q_local // kv_local
    adapter_rank_size = query_down_factor.shape[2]
    requests = lengths.shape[1]
    group_len = lengths[0]
    row_ids = exp_index * query_rows + jnp.arange(query_rows, dtype=jnp.int32)
    request, member, position = locate(row_ids, group_len)
    wanted = lax.dynamic_index_in_dim(request_adapter, req_index, 0, keepdims=False)
    slot_ids = jnp.arange(adapter_home_row.shape[0], dtype=jnp.int32)
    home_of = jnp.sum(
        jnp.where(wanted[:, None] == slot_ids[None, :], adapter_home_row[None, :], 0), axis=1
    )
    query_cols = q_local * HEAD_WIDTH
    kv_cols = kv_local * HEAD_WIDTH
    bank_local = query_down_factor.shape[0]
    up_q = lax.dynamic_slice_in_dim(query_up_factor, hid_index * query_cols, query_cols, 2)
    up_v = lax.dynamic_slice_in_dim(value_up_factor, hid_index * kv_cols, kv_cols, 2)
    parts_in = (query_down_factor, up_q, value_down_factor, up_v)
    part_shapes = [p.shape[1:] for p in parts_in]
    part_sizes = [p.shape[1] * p.shape[2] for p in parts_in]
    bank = jnp.concatenate([p.reshape(bank_local, -1) for p in parts_in], axis=1)
    along_req = lax.all_gather(bank, "req", axis=0, tiled=True)
    home_dev = home_of // bank_local
    home_pick = (home_dev // exp_count) * bank_local + home_of % bank_local
    mine = (home_dev % exp_count) == exp_index
    rows_pick = jnp.take(along_req, home_pick, axis=0)
    rows_pick = jnp.where(mine[:, None], rows_pick, jnp.zeros_like(rows_pick))
    rows_pick = lax.psum(rows_pick, "exp")
    chosen = []
    start = 0
    for shape_in, size_in in zip(part_shapes, part_sizes):
        chosen.append(rows_pick[:, start:start + size_in].reshape((requests,) + shape_in))
        start += size_in
    qa_sel, qb_sel, va_sel, vb_sel = chosen
    normed_rows = rms_norm(layer_input_rows, attention_norm_gain)

    def low_rank_term(a_sel, b_sel, width_cols, offset):
        inner_terms = jnp.einsum(
            "td,jdr->tjr", normed_rows, a_sel, preferred_element_type=jnp.float32
        )
        inner_terms = (
            jnp.where(member[:, :, None], inner_terms, 0.0)
            .reshape(query_rows, requests * adapter_rank_size)
            .astype(jnp.bfloat16)
        )
        right_factor = b_sel.reshape(requests * adapter_rank_size, width_cols)
        return jnp.dot(inner_terms, right_factor, preferred_element_type=jnp.float32)

    query_matrix = jnp.dot(
        normed_rows, query_weight, preferred_element_type=jnp.float32
    ) + low_rank_term(qa_sel, qb_sel, query_cols, hid_index * query_cols)
    query_matrix = rotary(query_matrix.reshape(query_rows, q_local, HEAD_WIDTH), position).astype(
        jnp.bfloat16
    )
    query_matrix = query_matrix.reshape(query_rows, kv_local, group_share, HEAD_WIDTH)
    keys_own = jnp.dot(normed_rows, key_weight, preferred_element_type=jnp.float32)
    keys_own = (
        rotary(keys_own.reshape(query_rows, kv_local, HEAD_WIDTH), position)
        .astype(jnp.bfloat16)
        .reshape(query_rows, kv_cols)
    )
    values_own = jnp.dot(
        normed_rows, value_weight, preferred_element_type=jnp.float32
    ) + low_rank_term(va_sel, vb_sel, kv_cols, hid_index * kv_cols)
    values_own = values_own.astype(jnp.bfloat16)
    running_max = jnp.full((kv_local, group_share, query_rows), neg_large, jnp.float32)
    key_piece = lax.all_gather(keys_own, "exp", axis=0, tiled=True)
    value_piece = lax.all_gather(values_own, "exp", axis=0, tiled=True)
    piece_len = key_piece.shape[0]
    key_ids = jnp.arange(piece_len, dtype=jnp.int32)
    key_request = request_of(key_ids, group_len)
    allowed = (request[:, None] == key_request[None, :]) & (key_ids[None, :] <= row_ids[:, None])
    key_heads = key_piece.reshape(piece_len, kv_local, HEAD_WIDTH)
    value_heads = value_piece.reshape(piece_len, kv_local, HEAD_WIDTH)
    scores = (
        jnp.einsum("qkgh,nkh->kgqn", query_matrix, key_heads, preferred_element_type=jnp.float32)
        * scale_attn
    )
    scores = jnp.where(allowed[None, None], scores, neg_large)
    new_max = jnp.maximum(running_max, jnp.max(scores, axis=-1))
    weights = jnp.where(allowed[None, None], jnp.exp(scores - new_max[..., None]), 0.0)
    running_sum = jnp.sum(weights, axis=-1)
    running_out = jnp.einsum(
        "kgqn,nkh->kgqh",
        weights.astype(jnp.bfloat16),
        value_heads,
        preferred_element_type=jnp.float32,
    )
    running_max, running_sum, running_out = (new_max, running_sum, running_out)
    attended = (running_out / running_sum[..., None]).astype(jnp.bfloat16)
    attended = jnp.transpose(attended, (2, 0, 1, 3)).reshape(query_rows, query_cols)
    tok_rows = query_rows // hid_count
    attn_out = lax.psum_scatter(
        jnp.dot(attended, attention_output_weight, preferred_element_type=jnp.float32).astype(
            jnp.bfloat16
        ),
        "hid",
        scatter_dimension=0,
        tiled=True,
    )
    own_rows = lax.dynamic_slice_in_dim(layer_input_rows, hid_index * tok_rows, tok_rows, 0)
    mixed_rows = own_rows.astype(jnp.float32) + residual_mult * attn_out.astype(jnp.float32)
    normed_moe = rms_norm(mixed_rows, expert_norm_gain)
    local_exp = expert_gate_weight.shape[0]
    expert_count = local_exp * exp_count
    top_count = routes.shape[1]
    capacity = max(2, tok_rows // 4)
    flat_route = routes.reshape(tok_rows * top_count)
    route_hits = (flat_route[:, None] == jnp.arange(expert_count, dtype=jnp.int32)[None, :]).astype(
        jnp.int32
    )
    earlier = jnp.cumsum(route_hits, axis=0) - route_hits
    slot_pos = jnp.sum(earlier * route_hits, axis=1)
    slots = slot_pos * expert_count + flat_route
    slot_table = jnp.arange(capacity * expert_count, dtype=jnp.int32)
    placed = jnp.any(
        slot_table[:, None, None] == slots.reshape(tok_rows, top_count)[None], axis=2
    ).astype(jnp.bfloat16)
    outgoing = jnp.dot(placed, normed_moe, preferred_element_type=jnp.float32).astype(jnp.bfloat16)
    outgoing = outgoing.reshape(capacity, expert_count, width)
    copies = jnp.broadcast_to(
        outgoing.reshape(capacity, exp_count, 1, local_exp, width),
        (capacity, exp_count, hid_count, local_exp, width),
    )
    copies = copies.reshape(capacity, exp_count * hid_count * local_exp, width)
    arrived = lax.all_to_all(copies, ("exp", "hid"), split_axis=1, concat_axis=0, tiled=True)
    partials = expert_rows(
        arrived, expert_gate_weight, expert_up_weight, expert_down_weight
    ).astype(jnp.bfloat16)
    partners = exp_count * hid_count
    partials = jnp.transpose(
        partials.reshape(partners, capacity, local_exp, width), (1, 0, 2, 3)
    ).reshape(capacity, partners * local_exp, width)
    returned = lax.all_to_all(partials, ("exp", "hid"), split_axis=1, concat_axis=1, tiled=True)
    returned = returned.reshape(capacity, exp_count, hid_count, local_exp, width)
    results = jnp.sum(returned.astype(jnp.float32), axis=2).astype(jnp.bfloat16)
    results = results.reshape(capacity * expert_count, width)
    picked = jnp.take(results, slots, axis=0).reshape(tok_rows, top_count, width)
    expert_out = jnp.sum(
        router_expert_weight[:, :, None] * picked.astype(jnp.float32), axis=1
    ).astype(jnp.bfloat16)
    return (attn_out, expert_out)


def solution(mesh):
    in_specs = (
        P(("req", "exp"), None),
        P(),
        P(None, "hid"),
        P(None, "hid"),
        P(None, "hid"),
        P("hid", None),
        P(("req", "exp"), None, None),
        P(("req", "exp"), None, None),
        P(("req", "exp"), None, None),
        P(("req", "exp"), None, None),
        P("req", None),
        P(),
        P(),
        P(),
        P(("req", "exp", "hid"), None),
        P(("req", "exp", "hid"), None),
        P("exp", None, "hid"),
        P("exp", None, "hid"),
        P("exp", "hid", None),
    )
    out_specs = (P(("req", "exp", "hid"), None), P(("req", "exp", "hid"), None))
    return jax.shard_map(
        per_device, mesh=mesh, in_specs=in_specs, out_specs=out_specs, check_vma=False
    )
```

```python
import jax
import jax.numpy as jnp
from jax import lax
from jax.sharding import PartitionSpec as P

HEAD_WIDTH = 64


scale_attn = 0.015625
residual_mult = 0.22
norm_eps = 1e-06
rope_base = 10000.0
neg_large = -1e30


def rms_norm(values, norm_gain):
    widened = values.astype(jnp.float32)
    mean_sq = jnp.mean(widened * widened, axis=-1, keepdims=True)
    return (widened * lax.rsqrt(mean_sq + norm_eps) * norm_gain).astype(jnp.bfloat16)


def rotary(heads_in, position):
    half_size = heads_in.shape[-1] // 2
    frequency = rope_base ** (-2.0 * jnp.arange(half_size, dtype=jnp.float32) / heads_in.shape[-1])
    angles = position.astype(jnp.float32)[:, None] * frequency[None, :]
    cosine = jnp.cos(angles)[:, None, :]
    sine_part = jnp.sin(angles)[:, None, :]
    first_half = heads_in[..., :half_size]
    second_half = heads_in[..., half_size:]
    return jnp.concatenate(
        [
            first_half * cosine - second_half * sine_part,
            second_half * cosine + first_half * sine_part,
        ],
        axis=-1,
    )


def request_of(row_ids, group_len):
    request_end = jnp.cumsum(group_len)
    return jnp.sum((row_ids[:, None] >= request_end[None, :]).astype(jnp.int32), axis=1)


def locate(row_ids, group_len):
    request_end = jnp.cumsum(group_len)
    request_start = request_end - group_len
    request = request_of(row_ids, group_len)
    member = request[:, None] == jnp.arange(group_len.shape[0], dtype=jnp.int32)[None, :]
    position = row_ids - jnp.sum(jnp.where(member, request_start[None, :], 0), axis=1)
    return (request, member, position)


def expert_rows(rows_in, expert_gate_weight, expert_up_weight, expert_down_weight):
    gate_act = jnp.einsum(
        "red,edf->ref", rows_in, expert_gate_weight, preferred_element_type=jnp.float32
    )
    upper = jnp.einsum(
        "red,edf->ref", rows_in, expert_up_weight, preferred_element_type=jnp.float32
    )
    hidden = (jax.nn.silu(gate_act) * upper).astype(jnp.bfloat16)
    return jnp.einsum(
        "ref,efd->red", hidden, expert_down_weight, preferred_element_type=jnp.float32
    )


def per_device(
    layer_input_rows,
    attention_norm_gain,
    query_weight,
    key_weight,
    value_weight,
    attention_output_weight,
    query_down_factor,
    query_up_factor,
    value_down_factor,
    value_up_factor,
    lengths,
    request_adapter,
    adapter_home_row,
    expert_norm_gain,
    routes,
    router_expert_weight,
    expert_gate_weight,
    expert_up_weight,
    expert_down_weight,
):
    exp_count = lax.axis_size("exp")
    hid_count = lax.axis_size("hid")
    exp_index = lax.axis_index("exp")
    hid_index = lax.axis_index("hid")
    req_index = lax.axis_index("req")
    query_rows = layer_input_rows.shape[0]
    width = layer_input_rows.shape[1]
    kv_local = key_weight.shape[1] // HEAD_WIDTH
    q_local = query_weight.shape[1] // HEAD_WIDTH
    group_share = q_local // kv_local
    adapter_rank_size = query_down_factor.shape[2]
    requests = lengths.shape[1]
    group_len = lengths[0]
    row_ids = exp_index * query_rows + jnp.arange(query_rows, dtype=jnp.int32)
    request, member, position = locate(row_ids, group_len)
    wanted = lax.dynamic_index_in_dim(request_adapter, req_index, 0, keepdims=False)
    slot_ids = jnp.arange(adapter_home_row.shape[0], dtype=jnp.int32)
    home_of = jnp.sum(
        jnp.where(wanted[:, None] == slot_ids[None, :], adapter_home_row[None, :], 0), axis=1
    )
    query_cols = q_local * HEAD_WIDTH
    kv_cols = kv_local * HEAD_WIDTH
    bank_local = query_down_factor.shape[0]
    up_q = lax.dynamic_slice_in_dim(query_up_factor, hid_index * query_cols, query_cols, 2)
    up_v = lax.dynamic_slice_in_dim(value_up_factor, hid_index * kv_cols, kv_cols, 2)
    down_rows = width // hid_count
    down_q = lax.dynamic_slice_in_dim(query_down_factor, hid_index * down_rows, down_rows, 1)
    down_v = lax.dynamic_slice_in_dim(value_down_factor, hid_index * down_rows, down_rows, 1)
    parts_in = (down_q, up_q, down_v, up_v)
    part_shapes = [p.shape[1:] for p in parts_in]
    part_sizes = [p.shape[1] * p.shape[2] for p in parts_in]
    bank = jnp.concatenate([p.reshape(bank_local, -1) for p in parts_in], axis=1)
    along_req = lax.all_gather(bank, "req", axis=0, tiled=True)
    home_dev = home_of // bank_local
    home_pick = (home_dev // exp_count) * bank_local + home_of % bank_local
    mine = (home_dev % exp_count) == exp_index
    rows_pick = jnp.take(along_req, home_pick, axis=0)
    rows_pick = jnp.where(mine[:, None], rows_pick, jnp.zeros_like(rows_pick))
    rows_pick = lax.psum(rows_pick, "exp")
    chosen = []
    start = 0
    for shape_in, size_in in zip(part_shapes, part_sizes):
        chosen.append(rows_pick[:, start:start + size_in].reshape((requests,) + shape_in))
        start += size_in
    qa_sel, qb_sel, va_sel, vb_sel = chosen
    normed_rows = rms_norm(layer_input_rows, attention_norm_gain)

    normed_slice = lax.dynamic_slice_in_dim(normed_rows, hid_index * down_rows, down_rows, 1)

    def inner_part(a_sel):
        inner_terms = jnp.einsum(
            "td,jdr->tjr", normed_slice, a_sel, preferred_element_type=jnp.float32
        )
        return jnp.sum(jnp.where(member[:, :, None], inner_terms, 0.0), axis=1)

    inner_both = lax.psum(
        jnp.concatenate([inner_part(qa_sel), inner_part(va_sel)], axis=1), "hid"
    ).astype(jnp.bfloat16)

    def low_rank_term(inner_own, b_sel, width_cols):
        inner_terms = jnp.where(member[:, :, None], inner_own[:, None, :], jnp.zeros_like(inner_own[:, None, :]))
        inner_terms = inner_terms.reshape(query_rows, requests * adapter_rank_size)
        right_factor = b_sel.reshape(requests * adapter_rank_size, width_cols)
        return jnp.dot(inner_terms, right_factor, preferred_element_type=jnp.float32)

    query_matrix = jnp.dot(
        normed_rows, query_weight, preferred_element_type=jnp.float32
    ) + low_rank_term(inner_both[:, :adapter_rank_size], qb_sel, query_cols)
    query_matrix = rotary(query_matrix.reshape(query_rows, q_local, HEAD_WIDTH), position).astype(
        jnp.bfloat16
    )
    query_matrix = query_matrix.reshape(query_rows, kv_local, group_share, HEAD_WIDTH)
    keys_own = jnp.dot(normed_rows, key_weight, preferred_element_type=jnp.float32)
    keys_own = (
        rotary(keys_own.reshape(query_rows, kv_local, HEAD_WIDTH), position)
        .astype(jnp.bfloat16)
        .reshape(query_rows, kv_cols)
    )
    values_own = jnp.dot(
        normed_rows, value_weight, preferred_element_type=jnp.float32
    ) + low_rank_term(inner_both[:, adapter_rank_size:], vb_sel, kv_cols)
    values_own = values_own.astype(jnp.bfloat16)
    running_max = jnp.full((kv_local, group_share, query_rows), neg_large, jnp.float32)
    key_piece = lax.all_gather(keys_own, "exp", axis=0, tiled=True)
    value_piece = lax.all_gather(values_own, "exp", axis=0, tiled=True)
    piece_len = key_piece.shape[0]
    key_ids = jnp.arange(piece_len, dtype=jnp.int32)
    key_request = request_of(key_ids, group_len)
    allowed = (request[:, None] == key_request[None, :]) & (key_ids[None, :] <= row_ids[:, None])
    key_heads = key_piece.reshape(piece_len, kv_local, HEAD_WIDTH)
    value_heads = value_piece.reshape(piece_len, kv_local, HEAD_WIDTH)
    scores = (
        jnp.einsum("qkgh,nkh->kgqn", query_matrix, key_heads, preferred_element_type=jnp.float32)
        * scale_attn
    )
    scores = jnp.where(allowed[None, None], scores, neg_large)
    new_max = jnp.maximum(running_max, jnp.max(scores, axis=-1))
    weights = jnp.where(allowed[None, None], jnp.exp(scores - new_max[..., None]), 0.0)
    running_sum = jnp.sum(weights, axis=-1)
    running_out = jnp.einsum(
        "kgqn,nkh->kgqh",
        weights.astype(jnp.bfloat16),
        value_heads,
        preferred_element_type=jnp.float32,
    )
    running_max, running_sum, running_out = (new_max, running_sum, running_out)
    attended = (running_out / running_sum[..., None]).astype(jnp.bfloat16)
    attended = jnp.transpose(attended, (2, 0, 1, 3)).reshape(query_rows, query_cols)
    tok_rows = query_rows // hid_count
    attn_out = lax.psum_scatter(
        jnp.dot(attended, attention_output_weight, preferred_element_type=jnp.float32).astype(
            jnp.bfloat16
        ),
        "hid",
        scatter_dimension=0,
        tiled=True,
    )
    own_rows = lax.dynamic_slice_in_dim(layer_input_rows, hid_index * tok_rows, tok_rows, 0)
    mixed_rows = own_rows.astype(jnp.float32) + residual_mult * attn_out.astype(jnp.float32)
    normed_moe = rms_norm(mixed_rows, expert_norm_gain)
    local_exp = expert_gate_weight.shape[0]
    expert_count = local_exp * exp_count
    top_count = routes.shape[1]
    capacity = max(2, tok_rows // 4)
    flat_route = routes.reshape(tok_rows * top_count)
    route_hits = (flat_route[:, None] == jnp.arange(expert_count, dtype=jnp.int32)[None, :]).astype(
        jnp.int32
    )
    earlier = jnp.cumsum(route_hits, axis=0) - route_hits
    slot_pos = jnp.sum(earlier * route_hits, axis=1)
    slots = slot_pos * expert_count + flat_route
    slot_table = jnp.arange(capacity * expert_count, dtype=jnp.int32)
    placed = jnp.any(
        slot_table[:, None, None] == slots.reshape(tok_rows, top_count)[None], axis=2
    ).astype(jnp.bfloat16)
    outgoing = jnp.dot(placed, normed_moe, preferred_element_type=jnp.float32).astype(jnp.bfloat16)
    outgoing = outgoing.reshape(capacity, expert_count, width)
    copies = jnp.broadcast_to(
        outgoing.reshape(capacity, exp_count, 1, local_exp, width),
        (capacity, exp_count, hid_count, local_exp, width),
    )
    copies = copies.reshape(capacity, exp_count * hid_count * local_exp, width)
    arrived = lax.all_to_all(copies, ("exp", "hid"), split_axis=1, concat_axis=0, tiled=True)
    partials = expert_rows(
        arrived, expert_gate_weight, expert_up_weight, expert_down_weight
    ).astype(jnp.bfloat16)
    partners = exp_count * hid_count
    partials = jnp.transpose(
        partials.reshape(partners, capacity, local_exp, width), (1, 0, 2, 3)
    ).reshape(capacity, partners * local_exp, width)
    returned = lax.all_to_all(partials, ("exp", "hid"), split_axis=1, concat_axis=1, tiled=True)
    returned = returned.reshape(capacity, exp_count, hid_count, local_exp, width)
    results = jnp.sum(returned.astype(jnp.float32), axis=2).astype(jnp.bfloat16)
    results = results.reshape(capacity * expert_count, width)
    picked = jnp.take(results, slots, axis=0).reshape(tok_rows, top_count, width)
    expert_out = jnp.sum(
        router_expert_weight[:, :, None] * picked.astype(jnp.float32), axis=1
    ).astype(jnp.bfloat16)
    return (attn_out, expert_out)


def solution(mesh):
    in_specs = (
        P(("req", "exp"), None),
        P(),
        P(None, "hid"),
        P(None, "hid"),
        P(None, "hid"),
        P("hid", None),
        P(("req", "exp"), None, None),
        P(("req", "exp"), None, None),
        P(("req", "exp"), None, None),
        P(("req", "exp"), None, None),
        P("req", None),
        P(),
        P(),
        P(),
        P(("req", "exp", "hid"), None),
        P(("req", "exp", "hid"), None),
        P("exp", None, "hid"),
        P("exp", None, "hid"),
        P("exp", "hid", None),
    )
    out_specs = (P(("req", "exp", "hid"), None), P(("req", "exp", "hid"), None))
    return jax.shard_map(
        per_device, mesh=mesh, in_specs=in_specs, out_specs=out_specs, check_vma=False
    )
```

```python
import jax
import jax.numpy as jnp
from jax import lax
from jax.sharding import PartitionSpec as P

HEAD_WIDTH = 64


scale_attn = 0.015625
residual_mult = 0.22
norm_eps = 1e-06
rope_base = 10000.0
neg_large = -1e30


def rms_norm(values, norm_gain):
    widened = values.astype(jnp.float32)
    mean_sq = jnp.mean(widened * widened, axis=-1, keepdims=True)
    return (widened * lax.rsqrt(mean_sq + norm_eps) * norm_gain).astype(jnp.bfloat16)


def rotary(heads_in, position):
    half_size = heads_in.shape[-1] // 2
    frequency = rope_base ** (-2.0 * jnp.arange(half_size, dtype=jnp.float32) / heads_in.shape[-1])
    angles = position.astype(jnp.float32)[:, None] * frequency[None, :]
    cosine = jnp.cos(angles)[:, None, :]
    sine_part = jnp.sin(angles)[:, None, :]
    first_half = heads_in[..., :half_size]
    second_half = heads_in[..., half_size:]
    return jnp.concatenate(
        [
            first_half * cosine - second_half * sine_part,
            second_half * cosine + first_half * sine_part,
        ],
        axis=-1,
    )


def request_of(row_ids, group_len):
    request_end = jnp.cumsum(group_len)
    return jnp.sum((row_ids[:, None] >= request_end[None, :]).astype(jnp.int32), axis=1)


def locate(row_ids, group_len):
    request_end = jnp.cumsum(group_len)
    request_start = request_end - group_len
    request = request_of(row_ids, group_len)
    member = request[:, None] == jnp.arange(group_len.shape[0], dtype=jnp.int32)[None, :]
    position = row_ids - jnp.sum(jnp.where(member, request_start[None, :], 0), axis=1)
    return (request, member, position)


def expert_rows(rows_in, expert_gate_weight, expert_up_weight, expert_down_weight):
    gate_act = jnp.einsum(
        "red,edf->ref", rows_in, expert_gate_weight, preferred_element_type=jnp.float32
    )
    upper = jnp.einsum(
        "red,edf->ref", rows_in, expert_up_weight, preferred_element_type=jnp.float32
    )
    hidden = (jax.nn.silu(gate_act) * upper).astype(jnp.bfloat16)
    return jnp.einsum(
        "ref,efd->red", hidden, expert_down_weight, preferred_element_type=jnp.float32
    )


def per_device(
    layer_input_rows,
    attention_norm_gain,
    query_weight,
    key_weight,
    value_weight,
    attention_output_weight,
    query_down_factor,
    query_up_factor,
    value_down_factor,
    value_up_factor,
    lengths,
    request_adapter,
    adapter_home_row,
    expert_norm_gain,
    routes,
    router_expert_weight,
    expert_gate_weight,
    expert_up_weight,
    expert_down_weight,
):
    exp_count = lax.axis_size("exp")
    hid_count = lax.axis_size("hid")
    exp_index = lax.axis_index("exp")
    hid_index = lax.axis_index("hid")
    req_index = lax.axis_index("req")
    query_rows = layer_input_rows.shape[0]
    width = layer_input_rows.shape[1]
    kv_local = key_weight.shape[1] // HEAD_WIDTH
    q_local = query_weight.shape[1] // HEAD_WIDTH
    group_share = q_local // kv_local
    adapter_rank_size = query_down_factor.shape[2]
    requests = lengths.shape[1]
    group_len = lengths[0]
    row_ids = exp_index * query_rows + jnp.arange(query_rows, dtype=jnp.int32)
    request, member, position = locate(row_ids, group_len)
    wanted = lax.dynamic_index_in_dim(request_adapter, req_index, 0, keepdims=False)
    slot_ids = jnp.arange(adapter_home_row.shape[0], dtype=jnp.int32)
    home_of = jnp.sum(
        jnp.where(wanted[:, None] == slot_ids[None, :], adapter_home_row[None, :], 0), axis=1
    )
    query_cols = q_local * HEAD_WIDTH
    kv_cols = kv_local * HEAD_WIDTH
    bank_local = query_down_factor.shape[0]
    up_q = lax.dynamic_slice_in_dim(query_up_factor, hid_index * query_cols, query_cols, 2)
    up_v = lax.dynamic_slice_in_dim(value_up_factor, hid_index * kv_cols, kv_cols, 2)
    parts_in = (query_down_factor, up_q, value_down_factor, up_v)
    part_shapes = [p.shape[1:] for p in parts_in]
    part_sizes = [p.shape[1] * p.shape[2] for p in parts_in]
    bank = jnp.concatenate([p.reshape(bank_local, -1) for p in parts_in], axis=1)
    along_req = lax.all_gather(bank, "req", axis=0, tiled=True)
    home_dev = home_of // bank_local
    home_pick = (home_dev // exp_count) * bank_local + home_of % bank_local
    mine = (home_dev % exp_count) == exp_index
    rows_pick = jnp.take(along_req, home_pick, axis=0)
    rows_pick = jnp.where(mine[:, None], rows_pick, jnp.zeros_like(rows_pick))
    rows_pick = jnp.sum(
        lax.all_to_all(
            jnp.broadcast_to(rows_pick[None], (exp_count,) + rows_pick.shape),
            "exp",
            split_axis=0,
            concat_axis=0,
            tiled=True,
        ).astype(jnp.float32),
        axis=0,
    ).astype(jnp.bfloat16)
    chosen = []
    start = 0
    for shape_in, size_in in zip(part_shapes, part_sizes):
        chosen.append(rows_pick[:, start:start + size_in].reshape((requests,) + shape_in))
        start += size_in
    qa_sel, qb_sel, va_sel, vb_sel = chosen
    normed_rows = rms_norm(layer_input_rows, attention_norm_gain)

    def low_rank_term(a_sel, b_sel, width_cols, offset):
        inner_terms = jnp.einsum(
            "td,jdr->tjr", normed_rows, a_sel, preferred_element_type=jnp.float32
        )
        inner_terms = (
            jnp.where(member[:, :, None], inner_terms, 0.0)
            .reshape(query_rows, requests * adapter_rank_size)
            .astype(jnp.bfloat16)
        )
        right_factor = b_sel.reshape(requests * adapter_rank_size, width_cols)
        return jnp.dot(inner_terms, right_factor, preferred_element_type=jnp.float32)

    query_matrix = jnp.dot(
        normed_rows, query_weight, preferred_element_type=jnp.float32
    ) + low_rank_term(qa_sel, qb_sel, query_cols, hid_index * query_cols)
    query_matrix = rotary(query_matrix.reshape(query_rows, q_local, HEAD_WIDTH), position).astype(
        jnp.bfloat16
    )
    query_matrix = query_matrix.reshape(query_rows, kv_local, group_share, HEAD_WIDTH)
    keys_own = jnp.dot(normed_rows, key_weight, preferred_element_type=jnp.float32)
    keys_own = (
        rotary(keys_own.reshape(query_rows, kv_local, HEAD_WIDTH), position)
        .astype(jnp.bfloat16)
        .reshape(query_rows, kv_cols)
    )
    values_own = jnp.dot(
        normed_rows, value_weight, preferred_element_type=jnp.float32
    ) + low_rank_term(va_sel, vb_sel, kv_cols, hid_index * kv_cols)
    values_own = values_own.astype(jnp.bfloat16)
    running_max = jnp.full((kv_local, group_share, query_rows), neg_large, jnp.float32)
    key_piece = lax.all_gather(keys_own, "exp", axis=0, tiled=True)
    value_piece = lax.all_gather(values_own, "exp", axis=0, tiled=True)
    piece_len = key_piece.shape[0]
    key_ids = jnp.arange(piece_len, dtype=jnp.int32)
    key_request = request_of(key_ids, group_len)
    allowed = (request[:, None] == key_request[None, :]) & (key_ids[None, :] <= row_ids[:, None])
    key_heads = key_piece.reshape(piece_len, kv_local, HEAD_WIDTH)
    value_heads = value_piece.reshape(piece_len, kv_local, HEAD_WIDTH)
    scores = (
        jnp.einsum("qkgh,nkh->kgqn", query_matrix, key_heads, preferred_element_type=jnp.float32)
        * scale_attn
    )
    scores = jnp.where(allowed[None, None], scores, neg_large)
    new_max = jnp.maximum(running_max, jnp.max(scores, axis=-1))
    weights = jnp.where(allowed[None, None], jnp.exp(scores - new_max[..., None]), 0.0)
    running_sum = jnp.sum(weights, axis=-1)
    running_out = jnp.einsum(
        "kgqn,nkh->kgqh",
        weights.astype(jnp.bfloat16),
        value_heads,
        preferred_element_type=jnp.float32,
    )
    running_max, running_sum, running_out = (new_max, running_sum, running_out)
    attended = (running_out / running_sum[..., None]).astype(jnp.bfloat16)
    attended = jnp.transpose(attended, (2, 0, 1, 3)).reshape(query_rows, query_cols)
    tok_rows = query_rows // hid_count
    head_sums = jnp.dot(attended, attention_output_weight, preferred_element_type=jnp.float32)
    head_sums = head_sums.astype(jnp.bfloat16).reshape(hid_count, tok_rows, width)
    head_sums = lax.all_to_all(head_sums, "hid", split_axis=0, concat_axis=0, tiled=True)
    attn_out = jnp.sum(head_sums.astype(jnp.float32), axis=0).astype(jnp.bfloat16)
    own_rows = lax.dynamic_slice_in_dim(layer_input_rows, hid_index * tok_rows, tok_rows, 0)
    mixed_rows = own_rows.astype(jnp.float32) + residual_mult * attn_out.astype(jnp.float32)
    normed_moe = rms_norm(mixed_rows, expert_norm_gain)
    local_exp = expert_gate_weight.shape[0]
    expert_count = local_exp * exp_count
    top_count = routes.shape[1]
    capacity = max(2, tok_rows // 4)
    flat_route = routes.reshape(tok_rows * top_count)
    route_hits = (flat_route[:, None] == jnp.arange(expert_count, dtype=jnp.int32)[None, :]).astype(
        jnp.int32
    )
    earlier = jnp.cumsum(route_hits, axis=0) - route_hits
    slot_pos = jnp.sum(earlier * route_hits, axis=1)
    slots = slot_pos * expert_count + flat_route
    slot_table = jnp.arange(capacity * expert_count, dtype=jnp.int32)
    placed = jnp.any(
        slot_table[:, None, None] == slots.reshape(tok_rows, top_count)[None], axis=2
    ).astype(jnp.bfloat16)
    outgoing = jnp.dot(placed, normed_moe, preferred_element_type=jnp.float32).astype(jnp.bfloat16)
    outgoing = outgoing.reshape(capacity, expert_count, width)
    copies = jnp.broadcast_to(
        outgoing.reshape(capacity, exp_count, 1, local_exp, width),
        (capacity, exp_count, hid_count, local_exp, width),
    )
    copies = copies.reshape(capacity, exp_count * hid_count * local_exp, width)
    arrived = lax.all_to_all(copies, ("exp", "hid"), split_axis=1, concat_axis=0, tiled=True)
    partials = expert_rows(
        arrived, expert_gate_weight, expert_up_weight, expert_down_weight
    ).astype(jnp.bfloat16)
    partners = exp_count * hid_count
    partials = jnp.transpose(
        partials.reshape(partners, capacity, local_exp, width), (1, 0, 2, 3)
    ).reshape(capacity, partners * local_exp, width)
    returned = lax.all_to_all(partials, ("exp", "hid"), split_axis=1, concat_axis=1, tiled=True)
    returned = returned.reshape(capacity, exp_count, hid_count, local_exp, width)
    results = jnp.sum(returned.astype(jnp.float32), axis=2).astype(jnp.bfloat16)
    results = results.reshape(capacity * expert_count, width)
    picked = jnp.take(results, slots, axis=0).reshape(tok_rows, top_count, width)
    expert_out = jnp.sum(
        router_expert_weight[:, :, None] * picked.astype(jnp.float32), axis=1
    ).astype(jnp.bfloat16)
    return (attn_out, expert_out)


def solution(mesh):
    in_specs = (
        P(("req", "exp"), None),
        P(),
        P(None, "hid"),
        P(None, "hid"),
        P(None, "hid"),
        P("hid", None),
        P(("req", "exp"), None, None),
        P(("req", "exp"), None, None),
        P(("req", "exp"), None, None),
        P(("req", "exp"), None, None),
        P("req", None),
        P(),
        P(),
        P(),
        P(("req", "exp", "hid"), None),
        P(("req", "exp", "hid"), None),
        P("exp", None, "hid"),
        P("exp", None, "hid"),
        P("exp", "hid", None),
    )
    out_specs = (P(("req", "exp", "hid"), None), P(("req", "exp", "hid"), None))
    return jax.shard_map(
        per_device, mesh=mesh, in_specs=in_specs, out_specs=out_specs, check_vma=False
    )
```

```python
import jax
import jax.numpy as jnp
from jax import lax
from jax.sharding import PartitionSpec as P

HEAD_WIDTH = 64


scale_attn = 0.015625
residual_mult = 0.22
norm_eps = 1e-06
rope_base = 10000.0
neg_large = -1e30


def rms_norm(values, norm_gain):
    widened = values.astype(jnp.float32)
    mean_sq = jnp.mean(widened * widened, axis=-1, keepdims=True)
    return (widened * lax.rsqrt(mean_sq + norm_eps) * norm_gain).astype(jnp.bfloat16)


def rotary(heads_in, position):
    half_size = heads_in.shape[-1] // 2
    frequency = rope_base ** (-2.0 * jnp.arange(half_size, dtype=jnp.float32) / heads_in.shape[-1])
    angles = position.astype(jnp.float32)[:, None] * frequency[None, :]
    cosine = jnp.cos(angles)[:, None, :]
    sine_part = jnp.sin(angles)[:, None, :]
    first_half = heads_in[..., :half_size]
    second_half = heads_in[..., half_size:]
    return jnp.concatenate(
        [
            first_half * cosine - second_half * sine_part,
            second_half * cosine + first_half * sine_part,
        ],
        axis=-1,
    )


def request_of(row_ids, group_len):
    request_end = jnp.cumsum(group_len)
    return jnp.sum((row_ids[:, None] >= request_end[None, :]).astype(jnp.int32), axis=1)


def locate(row_ids, group_len):
    request_end = jnp.cumsum(group_len)
    request_start = request_end - group_len
    request = request_of(row_ids, group_len)
    member = request[:, None] == jnp.arange(group_len.shape[0], dtype=jnp.int32)[None, :]
    position = row_ids - jnp.sum(jnp.where(member, request_start[None, :], 0), axis=1)
    return (request, member, position)


def expert_rows(rows_in, expert_gate_weight, expert_up_weight, expert_down_weight):
    gate_act = jnp.einsum(
        "red,edf->ref", rows_in, expert_gate_weight, preferred_element_type=jnp.float32
    )
    upper = jnp.einsum(
        "red,edf->ref", rows_in, expert_up_weight, preferred_element_type=jnp.float32
    )
    hidden = (jax.nn.silu(gate_act) * upper).astype(jnp.bfloat16)
    return jnp.einsum(
        "ref,efd->red", hidden, expert_down_weight, preferred_element_type=jnp.float32
    )


def per_device(
    layer_input_rows,
    attention_norm_gain,
    query_weight,
    key_weight,
    value_weight,
    attention_output_weight,
    query_down_factor,
    query_up_factor,
    value_down_factor,
    value_up_factor,
    lengths,
    request_adapter,
    adapter_home_row,
    expert_norm_gain,
    routes,
    router_expert_weight,
    expert_gate_weight,
    expert_up_weight,
    expert_down_weight,
):
    exp_count = lax.axis_size("exp")
    hid_count = lax.axis_size("hid")
    exp_index = lax.axis_index("exp")
    hid_index = lax.axis_index("hid")
    req_index = lax.axis_index("req")
    query_rows = layer_input_rows.shape[0]
    width = layer_input_rows.shape[1]
    kv_local = key_weight.shape[1] // HEAD_WIDTH
    q_local = query_weight.shape[1] // HEAD_WIDTH
    group_share = q_local // kv_local
    adapter_rank_size = query_down_factor.shape[2]
    requests = lengths.shape[1]
    group_len = lengths[0]
    row_ids = exp_index * query_rows + jnp.arange(query_rows, dtype=jnp.int32)
    request, member, position = locate(row_ids, group_len)
    wanted = lax.dynamic_index_in_dim(request_adapter, req_index, 0, keepdims=False)
    slot_ids = jnp.arange(adapter_home_row.shape[0], dtype=jnp.int32)
    home_of = jnp.sum(
        jnp.where(wanted[:, None] == slot_ids[None, :], adapter_home_row[None, :], 0), axis=1
    )
    query_cols = q_local * HEAD_WIDTH
    kv_cols = kv_local * HEAD_WIDTH
    bank_local = query_down_factor.shape[0]
    up_q = lax.dynamic_slice_in_dim(query_up_factor, hid_index * query_cols, query_cols, 2)
    up_v = lax.dynamic_slice_in_dim(value_up_factor, hid_index * kv_cols, kv_cols, 2)
    parts_in = (query_down_factor, up_q, value_down_factor, up_v)
    part_shapes = [p.shape[1:] for p in parts_in]
    part_sizes = [p.shape[1] * p.shape[2] for p in parts_in]
    bank = jnp.concatenate([p.reshape(bank_local, -1) for p in parts_in], axis=1)
    along_req = lax.all_gather(bank, "req", axis=0, tiled=True)
    home_dev = home_of // bank_local
    home_pick = (home_dev // exp_count) * bank_local + home_of % bank_local
    mine = (home_dev % exp_count) == exp_index
    rows_pick = jnp.take(along_req, home_pick, axis=0)
    rows_pick = jnp.where(mine[:, None], rows_pick, jnp.zeros_like(rows_pick))
    rows_all = lax.all_to_all(
        jnp.broadcast_to(rows_pick[None], (exp_count,) + rows_pick.shape),
        "exp",
        split_axis=0,
        concat_axis=0,
        tiled=True,
    )
    rows_pick = rows_all[home_dev % exp_count, jnp.arange(requests, dtype=jnp.int32)]
    chosen = []
    start = 0
    for shape_in, size_in in zip(part_shapes, part_sizes):
        chosen.append(rows_pick[:, start:start + size_in].reshape((requests,) + shape_in))
        start += size_in
    qa_sel, qb_sel, va_sel, vb_sel = chosen
    normed_rows = rms_norm(layer_input_rows, attention_norm_gain)

    def low_rank_term(a_sel, b_sel, width_cols, offset):
        inner_terms = jnp.einsum(
            "td,jdr->tjr", normed_rows, a_sel, preferred_element_type=jnp.float32
        )
        inner_terms = (
            jnp.where(member[:, :, None], inner_terms, 0.0)
            .reshape(query_rows, requests * adapter_rank_size)
            .astype(jnp.bfloat16)
        )
        right_factor = b_sel.reshape(requests * adapter_rank_size, width_cols)
        return jnp.dot(inner_terms, right_factor, preferred_element_type=jnp.float32)

    query_matrix = jnp.dot(
        normed_rows, query_weight, preferred_element_type=jnp.float32
    ) + low_rank_term(qa_sel, qb_sel, query_cols, hid_index * query_cols)
    query_matrix = rotary(query_matrix.reshape(query_rows, q_local, HEAD_WIDTH), position).astype(
        jnp.bfloat16
    )
    query_matrix = query_matrix.reshape(query_rows, kv_local, group_share, HEAD_WIDTH)
    keys_own = jnp.dot(normed_rows, key_weight, preferred_element_type=jnp.float32)
    keys_own = (
        rotary(keys_own.reshape(query_rows, kv_local, HEAD_WIDTH), position)
        .astype(jnp.bfloat16)
        .reshape(query_rows, kv_cols)
    )
    values_own = jnp.dot(
        normed_rows, value_weight, preferred_element_type=jnp.float32
    ) + low_rank_term(va_sel, vb_sel, kv_cols, hid_index * kv_cols)
    values_own = values_own.astype(jnp.bfloat16)
    running_max = jnp.full((kv_local, group_share, query_rows), neg_large, jnp.float32)
    key_piece = lax.all_gather(keys_own, "exp", axis=0, tiled=True)
    value_piece = lax.all_gather(values_own, "exp", axis=0, tiled=True)
    piece_len = key_piece.shape[0]
    key_ids = jnp.arange(piece_len, dtype=jnp.int32)
    key_request = request_of(key_ids, group_len)
    allowed = (request[:, None] == key_request[None, :]) & (key_ids[None, :] <= row_ids[:, None])
    key_heads = key_piece.reshape(piece_len, kv_local, HEAD_WIDTH)
    value_heads = value_piece.reshape(piece_len, kv_local, HEAD_WIDTH)
    scores = (
        jnp.einsum("qkgh,nkh->kgqn", query_matrix, key_heads, preferred_element_type=jnp.float32)
        * scale_attn
    )
    scores = jnp.where(allowed[None, None], scores, neg_large)
    new_max = jnp.maximum(running_max, jnp.max(scores, axis=-1))
    weights = jnp.where(allowed[None, None], jnp.exp(scores - new_max[..., None]), 0.0)
    running_sum = jnp.sum(weights, axis=-1)
    running_out = jnp.einsum(
        "kgqn,nkh->kgqh",
        weights.astype(jnp.bfloat16),
        value_heads,
        preferred_element_type=jnp.float32,
    )
    running_max, running_sum, running_out = (new_max, running_sum, running_out)
    attended = (running_out / running_sum[..., None]).astype(jnp.bfloat16)
    attended = jnp.transpose(attended, (2, 0, 1, 3)).reshape(query_rows, query_cols)
    tok_rows = query_rows // hid_count
    head_sums = jnp.dot(attended, attention_output_weight, preferred_element_type=jnp.float32)
    head_sums = head_sums.astype(jnp.bfloat16).reshape(hid_count, tok_rows, width)
    head_sums = lax.all_to_all(head_sums, "hid", split_axis=0, concat_axis=0, tiled=True)
    attn_out = jnp.sum(head_sums.astype(jnp.float32), axis=0).astype(jnp.bfloat16)
    own_rows = lax.dynamic_slice_in_dim(layer_input_rows, hid_index * tok_rows, tok_rows, 0)
    mixed_rows = own_rows.astype(jnp.float32) + residual_mult * attn_out.astype(jnp.float32)
    normed_moe = rms_norm(mixed_rows, expert_norm_gain)
    local_exp = expert_gate_weight.shape[0]
    expert_count = local_exp * exp_count
    top_count = routes.shape[1]
    capacity = max(2, tok_rows // 4)
    flat_route = routes.reshape(tok_rows * top_count)
    route_hits = (flat_route[:, None] == jnp.arange(expert_count, dtype=jnp.int32)[None, :]).astype(
        jnp.int32
    )
    earlier = jnp.cumsum(route_hits, axis=0) - route_hits
    slot_pos = jnp.sum(earlier * route_hits, axis=1)
    slots = slot_pos * expert_count + flat_route
    slot_table = jnp.arange(capacity * expert_count, dtype=jnp.int32)
    placed = jnp.any(
        slot_table[:, None, None] == slots.reshape(tok_rows, top_count)[None], axis=2
    ).astype(jnp.bfloat16)
    outgoing = jnp.dot(placed, normed_moe, preferred_element_type=jnp.float32).astype(jnp.bfloat16)
    outgoing = outgoing.reshape(capacity, expert_count, width)
    copies = jnp.broadcast_to(
        outgoing.reshape(capacity, exp_count, 1, local_exp, width),
        (capacity, exp_count, hid_count, local_exp, width),
    )
    copies = copies.reshape(capacity, exp_count * hid_count * local_exp, width)
    arrived = lax.all_to_all(copies, ("exp", "hid"), split_axis=1, concat_axis=0, tiled=True)
    partials = expert_rows(
        arrived, expert_gate_weight, expert_up_weight, expert_down_weight
    ).astype(jnp.bfloat16)
    partners = exp_count * hid_count
    partials = jnp.transpose(
        partials.reshape(partners, capacity, local_exp, width), (1, 0, 2, 3)
    ).reshape(capacity, partners * local_exp, width)
    returned = lax.all_to_all(partials, ("exp", "hid"), split_axis=1, concat_axis=1, tiled=True)
    returned = returned.reshape(capacity, exp_count, hid_count, local_exp, width)
    results = jnp.sum(returned.astype(jnp.float32), axis=2).astype(jnp.bfloat16)
    results = results.reshape(capacity * expert_count, width)
    slot_hit = slots.reshape(tok_rows, top_count)[:, :, None] == slot_table[None, None, :]
    combine = jnp.sum(
        jnp.where(slot_hit, router_expert_weight[:, :, None], 0.0), axis=1
    )
    expert_out = jnp.dot(
        combine,
        results.astype(jnp.float32),
        precision=lax.Precision.HIGHEST,
        preferred_element_type=jnp.float32,
    ).astype(jnp.bfloat16)
    return (attn_out, expert_out)


def solution(mesh):
    in_specs = (
        P(("req", "exp"), None),
        P(),
        P(None, "hid"),
        P(None, "hid"),
        P(None, "hid"),
        P("hid", None),
        P(("req", "exp"), None, None),
        P(("req", "exp"), None, None),
        P(("req", "exp"), None, None),
        P(("req", "exp"), None, None),
        P("req", None),
        P(),
        P(),
        P(),
        P(("req", "exp", "hid"), None),
        P(("req", "exp", "hid"), None),
        P("exp", None, "hid"),
        P("exp", None, "hid"),
        P("exp", "hid", None),
    )
    out_specs = (P(("req", "exp", "hid"), None), P(("req", "exp", "hid"), None))
    return jax.shard_map(
        per_device, mesh=mesh, in_specs=in_specs, out_specs=out_specs, check_vma=False
    )
```

```python
import jax
import jax.numpy as jnp
from jax import lax
from jax.sharding import PartitionSpec as P

HEAD_WIDTH = 64


scale_attn = 0.015625
residual_mult = 0.22
norm_eps = 1e-06
rope_base = 10000.0
neg_large = -1e30


def rms_norm(values, norm_gain):
    widened = values.astype(jnp.float32)
    mean_sq = jnp.mean(widened * widened, axis=-1, keepdims=True)
    return (widened * lax.rsqrt(mean_sq + norm_eps) * norm_gain).astype(jnp.bfloat16)


def rotary(heads_in, position):
    half_size = heads_in.shape[-1] // 2
    frequency = rope_base ** (-2.0 * jnp.arange(half_size, dtype=jnp.float32) / heads_in.shape[-1])
    angles = position.astype(jnp.float32)[:, None] * frequency[None, :]
    cosine = jnp.cos(angles)[:, None, :]
    sine_part = jnp.sin(angles)[:, None, :]
    first_half = heads_in[..., :half_size]
    second_half = heads_in[..., half_size:]
    return jnp.concatenate(
        [
            first_half * cosine - second_half * sine_part,
            second_half * cosine + first_half * sine_part,
        ],
        axis=-1,
    )


def request_of(row_ids, group_len):
    request_end = jnp.cumsum(group_len)
    return jnp.sum((row_ids[:, None] >= request_end[None, :]).astype(jnp.int32), axis=1)


def locate(row_ids, group_len):
    request_end = jnp.cumsum(group_len)
    request_start = request_end - group_len
    request = request_of(row_ids, group_len)
    member = request[:, None] == jnp.arange(group_len.shape[0], dtype=jnp.int32)[None, :]
    position = row_ids - jnp.sum(jnp.where(member, request_start[None, :], 0), axis=1)
    return (request, member, position)


def expert_rows(rows_in, expert_gate_weight, expert_up_weight, expert_down_weight):
    gate_act = jnp.einsum(
        "red,edf->ref", rows_in, expert_gate_weight, preferred_element_type=jnp.float32
    )
    upper = jnp.einsum(
        "red,edf->ref", rows_in, expert_up_weight, preferred_element_type=jnp.float32
    )
    hidden = (jax.nn.silu(gate_act) * upper).astype(jnp.bfloat16)
    return jnp.einsum(
        "ref,efd->red", hidden, expert_down_weight, preferred_element_type=jnp.float32
    )


def per_device(
    layer_input_rows,
    attention_norm_gain,
    query_weight,
    key_weight,
    value_weight,
    attention_output_weight,
    query_down_factor,
    query_up_factor,
    value_down_factor,
    value_up_factor,
    lengths,
    request_adapter,
    adapter_home_row,
    expert_norm_gain,
    routes,
    router_expert_weight,
    expert_gate_weight,
    expert_up_weight,
    expert_down_weight,
):
    exp_count = lax.axis_size("exp")
    hid_count = lax.axis_size("hid")
    exp_index = lax.axis_index("exp")
    hid_index = lax.axis_index("hid")
    req_index = lax.axis_index("req")
    query_rows = layer_input_rows.shape[0]
    width = layer_input_rows.shape[1]
    kv_local = key_weight.shape[1] // HEAD_WIDTH
    q_local = query_weight.shape[1] // HEAD_WIDTH
    group_share = q_local // kv_local
    adapter_rank_size = query_down_factor.shape[2]
    requests = lengths.shape[1]
    group_len = lengths[0]
    row_ids = exp_index * query_rows + jnp.arange(query_rows, dtype=jnp.int32)
    request, member, position = locate(row_ids, group_len)
    wanted = lax.dynamic_index_in_dim(request_adapter, req_index, 0, keepdims=False)
    slot_ids = jnp.arange(adapter_home_row.shape[0], dtype=jnp.int32)
    home_of = jnp.sum(
        jnp.where(wanted[:, None] == slot_ids[None, :], adapter_home_row[None, :], 0), axis=1
    )
    query_cols = q_local * HEAD_WIDTH
    kv_cols = kv_local * HEAD_WIDTH
    bank_local = query_down_factor.shape[0]
    up_q = lax.dynamic_slice_in_dim(query_up_factor, hid_index * query_cols, query_cols, 2)
    up_v = lax.dynamic_slice_in_dim(value_up_factor, hid_index * kv_cols, kv_cols, 2)
    parts_in = (query_down_factor, up_q, value_down_factor, up_v)
    part_shapes = [p.shape[1:] for p in parts_in]
    part_sizes = [p.shape[1] * p.shape[2] for p in parts_in]
    bank = jnp.concatenate([p.reshape(bank_local, -1) for p in parts_in], axis=1)
    along_req = lax.all_gather(bank, "req", axis=0, tiled=True)
    home_dev = home_of // bank_local
    home_pick = (home_dev // exp_count) * bank_local + home_of % bank_local
    mine = (home_dev % exp_count) == exp_index
    rows_pick = jnp.take(along_req, home_pick, axis=0)
    rows_pick = jnp.where(mine[:, None], rows_pick, jnp.zeros_like(rows_pick))
    rows_all = lax.all_to_all(
        jnp.broadcast_to(rows_pick[None], (exp_count,) + rows_pick.shape),
        "exp",
        split_axis=0,
        concat_axis=0,
        tiled=True,
    )
    rows_pick = rows_all[home_dev % exp_count, jnp.arange(requests, dtype=jnp.int32)]
    chosen = []
    start = 0
    for shape_in, size_in in zip(part_shapes, part_sizes):
        chosen.append(rows_pick[:, start:start + size_in].reshape((requests,) + shape_in))
        start += size_in
    qa_sel, qb_sel, va_sel, vb_sel = chosen
    normed_rows = rms_norm(layer_input_rows, attention_norm_gain)

    def low_rank_term(a_sel, b_sel, width_cols, offset):
        inner_terms = jnp.einsum(
            "td,jdr->tjr", normed_rows, a_sel, preferred_element_type=jnp.float32
        )
        inner_terms = (
            jnp.where(member[:, :, None], inner_terms, 0.0)
            .reshape(query_rows, requests * adapter_rank_size)
            .astype(jnp.bfloat16)
        )
        right_factor = b_sel.reshape(requests * adapter_rank_size, width_cols)
        return jnp.dot(inner_terms, right_factor, preferred_element_type=jnp.float32)

    query_matrix = jnp.dot(
        normed_rows, query_weight, preferred_element_type=jnp.float32
    ) + low_rank_term(qa_sel, qb_sel, query_cols, hid_index * query_cols)
    query_matrix = rotary(query_matrix.reshape(query_rows, q_local, HEAD_WIDTH), position).astype(
        jnp.bfloat16
    )
    query_matrix = query_matrix.reshape(query_rows, kv_local, group_share, HEAD_WIDTH)
    keys_own = jnp.dot(normed_rows, key_weight, preferred_element_type=jnp.float32)
    keys_own = (
        rotary(keys_own.reshape(query_rows, kv_local, HEAD_WIDTH), position)
        .astype(jnp.bfloat16)
        .reshape(query_rows, kv_cols)
    )
    values_own = jnp.dot(
        normed_rows, value_weight, preferred_element_type=jnp.float32
    ) + low_rank_term(va_sel, vb_sel, kv_cols, hid_index * kv_cols)
    values_own = values_own.astype(jnp.bfloat16)
    running_max = jnp.full((kv_local, group_share, query_rows), neg_large, jnp.float32)
    key_piece = lax.all_gather(keys_own, "exp", axis=0, tiled=True)
    value_piece = lax.all_gather(values_own, "exp", axis=0, tiled=True)
    piece_len = key_piece.shape[0]
    key_ids = jnp.arange(piece_len, dtype=jnp.int32)
    key_request = request_of(key_ids, group_len)
    allowed = (request[:, None] == key_request[None, :]) & (key_ids[None, :] <= row_ids[:, None])
    key_heads = key_piece.reshape(piece_len, kv_local, HEAD_WIDTH)
    value_heads = value_piece.reshape(piece_len, kv_local, HEAD_WIDTH)
    scores = (
        jnp.einsum("qkgh,nkh->kgqn", query_matrix, key_heads, preferred_element_type=jnp.float32)
        * scale_attn
    )
    scores = jnp.where(allowed[None, None], scores, neg_large)
    new_max = jnp.maximum(running_max, jnp.max(scores, axis=-1))
    weights = jnp.where(allowed[None, None], jnp.exp(scores - new_max[..., None]), 0.0)
    running_sum = jnp.sum(weights, axis=-1)
    running_out = jnp.einsum(
        "kgqn,nkh->kgqh",
        weights.astype(jnp.bfloat16),
        value_heads,
        preferred_element_type=jnp.float32,
    )
    running_max, running_sum, running_out = (new_max, running_sum, running_out)
    attended = (running_out / running_sum[..., None]).astype(jnp.bfloat16)
    attended = jnp.transpose(attended, (2, 0, 1, 3)).reshape(query_rows, query_cols)
    tok_rows = query_rows // hid_count
    head_sums = jnp.dot(attended, attention_output_weight, preferred_element_type=jnp.float32)
    head_sums = head_sums.astype(jnp.bfloat16).reshape(hid_count, tok_rows, width)
    head_sums = lax.all_to_all(head_sums, "hid", split_axis=0, concat_axis=0, tiled=True)
    attn_out = jnp.sum(head_sums.astype(jnp.float32), axis=0).astype(jnp.bfloat16)
    own_rows = lax.dynamic_slice_in_dim(layer_input_rows, hid_index * tok_rows, tok_rows, 0)
    mixed_rows = own_rows.astype(jnp.float32) + residual_mult * attn_out.astype(jnp.float32)
    normed_moe = rms_norm(mixed_rows, expert_norm_gain)
    local_exp = expert_gate_weight.shape[0]
    expert_count = local_exp * exp_count
    top_count = routes.shape[1]
    capacity = max(2, tok_rows // 4)
    flat_route = routes.reshape(tok_rows * top_count)
    route_hits = (flat_route[:, None] == jnp.arange(expert_count, dtype=jnp.int32)[None, :]).astype(
        jnp.int32
    )
    earlier = jnp.cumsum(route_hits, axis=0) - route_hits
    slot_pos = jnp.sum(earlier * route_hits, axis=1)
    slots = slot_pos * expert_count + flat_route
    slot_table = jnp.arange(capacity * expert_count, dtype=jnp.int32)
    placed = jnp.any(
        slot_table[:, None, None] == slots.reshape(tok_rows, top_count)[None], axis=2
    ).astype(jnp.bfloat16)
    outgoing = jnp.dot(placed, normed_moe, preferred_element_type=jnp.float32).astype(jnp.bfloat16)
    outgoing = outgoing.reshape(capacity, expert_count, width)
    partners = exp_count * hid_count
    halves = 2 if capacity % 2 == 0 else 1
    cap_part = capacity // halves
    slot_hit = slots.reshape(tok_rows, top_count)[:, :, None] == slot_table[None, None, :]
    combine = jnp.sum(jnp.where(slot_hit, router_expert_weight[:, :, None], 0.0), axis=1)
    expert_acc = jnp.zeros((tok_rows, width), jnp.float32)
    for half in range(halves):
        part_out = outgoing[half * cap_part:(half + 1) * cap_part]
        copies = jnp.broadcast_to(
            part_out.reshape(cap_part, exp_count, 1, local_exp, width),
            (cap_part, exp_count, hid_count, local_exp, width),
        )
        copies = copies.reshape(cap_part, partners * local_exp, width)
        arrived = lax.all_to_all(copies, ("exp", "hid"), split_axis=1, concat_axis=0, tiled=True)
        partials = expert_rows(
            arrived, expert_gate_weight, expert_up_weight, expert_down_weight
        ).astype(jnp.bfloat16)
        partials = jnp.transpose(
            partials.reshape(partners, cap_part, local_exp, width), (1, 0, 2, 3)
        ).reshape(cap_part, partners * local_exp, width)
        returned = lax.all_to_all(partials, ("exp", "hid"), split_axis=1, concat_axis=1, tiled=True)
        returned = returned.reshape(cap_part, exp_count, hid_count, local_exp, width)
        results = jnp.sum(returned.astype(jnp.float32), axis=2).astype(jnp.bfloat16)
        results = results.reshape(cap_part * expert_count, width)
        part_cols = combine[:, half * cap_part * expert_count:(half + 1) * cap_part * expert_count]
        expert_acc = expert_acc + jnp.dot(
            part_cols,
            results.astype(jnp.float32),
            precision=lax.Precision.HIGHEST,
            preferred_element_type=jnp.float32,
        )
    expert_out = expert_acc.astype(jnp.bfloat16)
    return (attn_out, expert_out)


def solution(mesh):
    in_specs = (
        P(("req", "exp"), None),
        P(),
        P(None, "hid"),
        P(None, "hid"),
        P(None, "hid"),
        P("hid", None),
        P(("req", "exp"), None, None),
        P(("req", "exp"), None, None),
        P(("req", "exp"), None, None),
        P(("req", "exp"), None, None),
        P("req", None),
        P(),
        P(),
        P(),
        P(("req", "exp", "hid"), None),
        P(("req", "exp", "hid"), None),
        P("exp", None, "hid"),
        P("exp", None, "hid"),
        P("exp", "hid", None),
    )
    out_specs = (P(("req", "exp", "hid"), None), P(("req", "exp", "hid"), None))
    return jax.shard_map(
        per_device, mesh=mesh, in_specs=in_specs, out_specs=out_specs, check_vma=False
    )
```

```python
import jax
import jax.numpy as jnp
from jax import lax
from jax.sharding import PartitionSpec as P

HEAD_WIDTH = 64


scale_attn = 0.015625
residual_mult = 0.22
norm_eps = 1e-06
rope_base = 10000.0
neg_large = -1e30


def rms_norm(values, norm_gain):
    widened = values.astype(jnp.float32)
    mean_sq = jnp.mean(widened * widened, axis=-1, keepdims=True)
    return (widened * lax.rsqrt(mean_sq + norm_eps) * norm_gain).astype(jnp.bfloat16)


def rotary(heads_in, position):
    half_size = heads_in.shape[-1] // 2
    frequency = rope_base ** (-2.0 * jnp.arange(half_size, dtype=jnp.float32) / heads_in.shape[-1])
    angles = position.astype(jnp.float32)[:, None] * frequency[None, :]
    cosine = jnp.cos(angles)[:, None, :]
    sine_part = jnp.sin(angles)[:, None, :]
    first_half = heads_in[..., :half_size]
    second_half = heads_in[..., half_size:]
    return jnp.concatenate(
        [
            first_half * cosine - second_half * sine_part,
            second_half * cosine + first_half * sine_part,
        ],
        axis=-1,
    )


def request_of(row_ids, group_len):
    request_end = jnp.cumsum(group_len)
    return jnp.sum((row_ids[:, None] >= request_end[None, :]).astype(jnp.int32), axis=1)


def locate(row_ids, group_len):
    request_end = jnp.cumsum(group_len)
    request_start = request_end - group_len
    request = request_of(row_ids, group_len)
    member = request[:, None] == jnp.arange(group_len.shape[0], dtype=jnp.int32)[None, :]
    position = row_ids - jnp.sum(jnp.where(member, request_start[None, :], 0), axis=1)
    return (request, member, position)


def expert_rows(rows_in, expert_gate_weight, expert_up_weight, expert_down_weight):
    gate_act = jnp.einsum(
        "red,edf->ref", rows_in, expert_gate_weight, preferred_element_type=jnp.float32
    )
    upper = jnp.einsum(
        "red,edf->ref", rows_in, expert_up_weight, preferred_element_type=jnp.float32
    )
    hidden = (jax.nn.silu(gate_act) * upper).astype(jnp.bfloat16)
    return jnp.einsum(
        "ref,efd->red", hidden, expert_down_weight, preferred_element_type=jnp.float32
    )


def per_device(
    layer_input_rows,
    attention_norm_gain,
    query_weight,
    key_weight,
    value_weight,
    attention_output_weight,
    query_down_factor,
    query_up_factor,
    value_down_factor,
    value_up_factor,
    lengths,
    request_adapter,
    adapter_home_row,
    expert_norm_gain,
    routes,
    router_expert_weight,
    expert_gate_weight,
    expert_up_weight,
    expert_down_weight,
):
    exp_count = lax.axis_size("exp")
    hid_count = lax.axis_size("hid")
    exp_index = lax.axis_index("exp")
    hid_index = lax.axis_index("hid")
    req_index = lax.axis_index("req")
    query_rows = layer_input_rows.shape[0]
    width = layer_input_rows.shape[1]
    kv_local = key_weight.shape[1] // HEAD_WIDTH
    q_local = query_weight.shape[1] // HEAD_WIDTH
    group_share = q_local // kv_local
    adapter_rank_size = query_down_factor.shape[2]
    requests = lengths.shape[1]
    group_len = lengths[0]
    row_ids = exp_index * query_rows + jnp.arange(query_rows, dtype=jnp.int32)
    request, member, position = locate(row_ids, group_len)
    wanted = lax.dynamic_index_in_dim(request_adapter, req_index, 0, keepdims=False)
    slot_ids = jnp.arange(adapter_home_row.shape[0], dtype=jnp.int32)
    home_of = jnp.sum(
        jnp.where(wanted[:, None] == slot_ids[None, :], adapter_home_row[None, :], 0), axis=1
    )
    query_cols = q_local * HEAD_WIDTH
    kv_cols = kv_local * HEAD_WIDTH
    bank_local = query_down_factor.shape[0]
    up_q = lax.dynamic_slice_in_dim(query_up_factor, hid_index * query_cols, query_cols, 2)
    up_v = lax.dynamic_slice_in_dim(value_up_factor, hid_index * kv_cols, kv_cols, 2)
    parts_in = (query_down_factor, up_q, value_down_factor, up_v)
    part_shapes = [p.shape[1:] for p in parts_in]
    part_sizes = [p.shape[1] * p.shape[2] for p in parts_in]
    bank = jnp.concatenate([p.reshape(bank_local, -1) for p in parts_in], axis=1)
    along_req = lax.all_gather(bank, "req", axis=0, tiled=True)
    home_dev = home_of // bank_local
    home_pick = (home_dev // exp_count) * bank_local + home_of % bank_local
    mine = (home_dev % exp_count) == exp_index
    rows_pick = jnp.take(along_req, home_pick, axis=0)
    rows_pick = jnp.where(mine[:, None], rows_pick, jnp.zeros_like(rows_pick))
    rows_all = lax.all_to_all(
        jnp.broadcast_to(rows_pick[None], (exp_count,) + rows_pick.shape),
        "exp",
        split_axis=0,
        concat_axis=0,
        tiled=True,
    )
    rows_pick = rows_all[home_dev % exp_count, jnp.arange(requests, dtype=jnp.int32)]
    chosen = []
    start = 0
    for shape_in, size_in in zip(part_shapes, part_sizes):
        chosen.append(rows_pick[:, start:start + size_in].reshape((requests,) + shape_in))
        start += size_in
    qa_sel, qb_sel, va_sel, vb_sel = chosen
    normed_rows = rms_norm(layer_input_rows, attention_norm_gain)

    def low_rank_term(a_sel, b_sel, width_cols, offset):
        inner_terms = jnp.einsum(
            "td,jdr->tjr", normed_rows, a_sel, preferred_element_type=jnp.float32
        )
        inner_terms = (
            jnp.where(member[:, :, None], inner_terms, 0.0)
            .reshape(query_rows, requests * adapter_rank_size)
            .astype(jnp.bfloat16)
        )
        right_factor = b_sel.reshape(requests * adapter_rank_size, width_cols)
        return jnp.dot(inner_terms, right_factor, preferred_element_type=jnp.float32)

    query_matrix = jnp.dot(
        normed_rows, query_weight, preferred_element_type=jnp.float32
    ) + low_rank_term(qa_sel, qb_sel, query_cols, hid_index * query_cols)
    query_matrix = rotary(query_matrix.reshape(query_rows, q_local, HEAD_WIDTH), position).astype(
        jnp.bfloat16
    )
    query_matrix = query_matrix.reshape(query_rows, kv_local, group_share, HEAD_WIDTH)
    keys_own = jnp.dot(normed_rows, key_weight, preferred_element_type=jnp.float32)
    keys_own = (
        rotary(keys_own.reshape(query_rows, kv_local, HEAD_WIDTH), position)
        .astype(jnp.bfloat16)
        .reshape(query_rows, kv_cols)
    )
    values_own = jnp.dot(
        normed_rows, value_weight, preferred_element_type=jnp.float32
    ) + low_rank_term(va_sel, vb_sel, kv_cols, hid_index * kv_cols)
    values_own = values_own.astype(jnp.bfloat16)
    running_max = jnp.full((kv_local, group_share, query_rows), neg_large, jnp.float32)
    kv_piece = lax.all_gather(
        jnp.concatenate([keys_own, values_own], axis=1), "exp", axis=0, tiled=True
    )
    key_piece = kv_piece[:, :kv_cols]
    value_piece = kv_piece[:, kv_cols:]
    piece_len = key_piece.shape[0]
    key_ids = jnp.arange(piece_len, dtype=jnp.int32)
    key_request = request_of(key_ids, group_len)
    allowed = (request[:, None] == key_request[None, :]) & (key_ids[None, :] <= row_ids[:, None])
    key_heads = key_piece.reshape(piece_len, kv_local, HEAD_WIDTH)
    value_heads = value_piece.reshape(piece_len, kv_local, HEAD_WIDTH)
    scores = (
        jnp.einsum("qkgh,nkh->kgqn", query_matrix, key_heads, preferred_element_type=jnp.float32)
        * scale_attn
    )
    scores = jnp.where(allowed[None, None], scores, neg_large)
    new_max = jnp.maximum(running_max, jnp.max(scores, axis=-1))
    weights = jnp.where(allowed[None, None], jnp.exp(scores - new_max[..., None]), 0.0)
    running_sum = jnp.sum(weights, axis=-1)
    running_out = jnp.einsum(
        "kgqn,nkh->kgqh",
        weights.astype(jnp.bfloat16),
        value_heads,
        preferred_element_type=jnp.float32,
    )
    running_max, running_sum, running_out = (new_max, running_sum, running_out)
    attended = (running_out / running_sum[..., None]).astype(jnp.bfloat16)
    attended = jnp.transpose(attended, (2, 0, 1, 3)).reshape(query_rows, query_cols)
    tok_rows = query_rows // hid_count
    head_sums = jnp.dot(attended, attention_output_weight, preferred_element_type=jnp.float32)
    head_sums = head_sums.astype(jnp.bfloat16).reshape(hid_count, tok_rows, width)
    head_sums = lax.all_to_all(head_sums, "hid", split_axis=0, concat_axis=0, tiled=True)
    attn_out = jnp.sum(head_sums.astype(jnp.float32), axis=0).astype(jnp.bfloat16)
    own_rows = lax.dynamic_slice_in_dim(layer_input_rows, hid_index * tok_rows, tok_rows, 0)
    mixed_rows = own_rows.astype(jnp.float32) + residual_mult * attn_out.astype(jnp.float32)
    normed_moe = rms_norm(mixed_rows, expert_norm_gain)
    local_exp = expert_gate_weight.shape[0]
    expert_count = local_exp * exp_count
    top_count = routes.shape[1]
    capacity = max(2, tok_rows // 4)
    flat_route = routes.reshape(tok_rows * top_count)
    route_hits = (flat_route[:, None] == jnp.arange(expert_count, dtype=jnp.int32)[None, :]).astype(
        jnp.int32
    )
    earlier = jnp.cumsum(route_hits, axis=0) - route_hits
    slot_pos = jnp.sum(earlier * route_hits, axis=1)
    slots = slot_pos * expert_count + flat_route
    slot_table = jnp.arange(capacity * expert_count, dtype=jnp.int32)
    placed = jnp.any(
        slot_table[:, None, None] == slots.reshape(tok_rows, top_count)[None], axis=2
    ).astype(jnp.bfloat16)
    outgoing = jnp.dot(placed, normed_moe, preferred_element_type=jnp.float32).astype(jnp.bfloat16)
    outgoing = outgoing.reshape(capacity, expert_count, width)
    partners = exp_count * hid_count
    halves = 2 if capacity % 2 == 0 else 1
    cap_part = capacity // halves
    slot_hit = slots.reshape(tok_rows, top_count)[:, :, None] == slot_table[None, None, :]
    combine = jnp.sum(jnp.where(slot_hit, router_expert_weight[:, :, None], 0.0), axis=1)
    expert_acc = jnp.zeros((tok_rows, width), jnp.float32)
    for half in range(halves):
        part_out = outgoing[half * cap_part:(half + 1) * cap_part]
        copies = jnp.broadcast_to(
            part_out.reshape(cap_part, exp_count, 1, local_exp, width),
            (cap_part, exp_count, hid_count, local_exp, width),
        )
        copies = copies.reshape(cap_part, partners * local_exp, width)
        arrived = lax.all_to_all(copies, ("exp", "hid"), split_axis=1, concat_axis=0, tiled=True)
        partials = expert_rows(
            arrived, expert_gate_weight, expert_up_weight, expert_down_weight
        ).astype(jnp.bfloat16)
        partials = jnp.transpose(
            partials.reshape(partners, cap_part, local_exp, width), (1, 0, 2, 3)
        ).reshape(cap_part, partners * local_exp, width)
        returned = lax.all_to_all(partials, ("exp", "hid"), split_axis=1, concat_axis=1, tiled=True)
        returned = returned.reshape(cap_part, exp_count, hid_count, local_exp, width)
        results = jnp.sum(returned.astype(jnp.float32), axis=2).astype(jnp.bfloat16)
        results = results.reshape(cap_part * expert_count, width)
        part_cols = combine[:, half * cap_part * expert_count:(half + 1) * cap_part * expert_count]
        expert_acc = expert_acc + jnp.dot(
            part_cols,
            results.astype(jnp.float32),
            precision=lax.Precision.HIGHEST,
            preferred_element_type=jnp.float32,
        )
    expert_out = expert_acc.astype(jnp.bfloat16)
    return (attn_out, expert_out)


def solution(mesh):
    in_specs = (
        P(("req", "exp"), None),
        P(),
        P(None, "hid"),
        P(None, "hid"),
        P(None, "hid"),
        P("hid", None),
        P(("req", "exp"), None, None),
        P(("req", "exp"), None, None),
        P(("req", "exp"), None, None),
        P(("req", "exp"), None, None),
        P("req", None),
        P(),
        P(),
        P(),
        P(("req", "exp", "hid"), None),
        P(("req", "exp", "hid"), None),
        P("exp", None, "hid"),
        P("exp", None, "hid"),
        P("exp", "hid", None),
    )
    out_specs = (P(("req", "exp", "hid"), None), P(("req", "exp", "hid"), None))
    return jax.shard_map(
        per_device, mesh=mesh, in_specs=in_specs, out_specs=out_specs, check_vma=False
    )
```

```python
import jax
import jax.numpy as jnp
from jax import lax
from jax.sharding import PartitionSpec as P

HEAD_WIDTH = 64


scale_attn = 0.015625
residual_mult = 0.22
norm_eps = 1e-06
rope_base = 10000.0
neg_large = -1e30


def rms_norm(values, norm_gain):
    widened = values.astype(jnp.float32)
    mean_sq = jnp.mean(widened * widened, axis=-1, keepdims=True)
    return (widened * lax.rsqrt(mean_sq + norm_eps) * norm_gain).astype(jnp.bfloat16)


def rotary(heads_in, position):
    half_size = heads_in.shape[-1] // 2
    frequency = rope_base ** (-2.0 * jnp.arange(half_size, dtype=jnp.float32) / heads_in.shape[-1])
    angles = position.astype(jnp.float32)[:, None] * frequency[None, :]
    cosine = jnp.cos(angles)[:, None, :]
    sine_part = jnp.sin(angles)[:, None, :]
    first_half = heads_in[..., :half_size]
    second_half = heads_in[..., half_size:]
    return jnp.concatenate(
        [
            first_half * cosine - second_half * sine_part,
            second_half * cosine + first_half * sine_part,
        ],
        axis=-1,
    )


def request_of(row_ids, group_len):
    request_end = jnp.cumsum(group_len)
    return jnp.sum((row_ids[:, None] >= request_end[None, :]).astype(jnp.int32), axis=1)


def locate(row_ids, group_len):
    request_end = jnp.cumsum(group_len)
    request_start = request_end - group_len
    request = request_of(row_ids, group_len)
    member = request[:, None] == jnp.arange(group_len.shape[0], dtype=jnp.int32)[None, :]
    position = row_ids - jnp.sum(jnp.where(member, request_start[None, :], 0), axis=1)
    return (request, member, position)


def expert_rows(rows_in, expert_gate_weight, expert_up_weight, expert_down_weight):
    gate_act = jnp.einsum(
        "red,edf->ref", rows_in, expert_gate_weight, preferred_element_type=jnp.float32
    )
    upper = jnp.einsum(
        "red,edf->ref", rows_in, expert_up_weight, preferred_element_type=jnp.float32
    )
    hidden = (jax.nn.silu(gate_act) * upper).astype(jnp.bfloat16)
    return jnp.einsum(
        "ref,efd->red", hidden, expert_down_weight, preferred_element_type=jnp.float32
    )


def per_device(
    layer_input_rows,
    attention_norm_gain,
    query_weight,
    key_weight,
    value_weight,
    attention_output_weight,
    query_down_factor,
    query_up_factor,
    value_down_factor,
    value_up_factor,
    lengths,
    request_adapter,
    adapter_home_row,
    expert_norm_gain,
    routes,
    router_expert_weight,
    expert_gate_weight,
    expert_up_weight,
    expert_down_weight,
):
    exp_count = lax.axis_size("exp")
    hid_count = lax.axis_size("hid")
    exp_index = lax.axis_index("exp")
    hid_index = lax.axis_index("hid")
    req_index = lax.axis_index("req")
    query_rows = layer_input_rows.shape[0]
    width = layer_input_rows.shape[1]
    kv_local = key_weight.shape[1] // HEAD_WIDTH
    q_local = query_weight.shape[1] // HEAD_WIDTH
    group_share = q_local // kv_local
    adapter_rank_size = query_down_factor.shape[2]
    requests = lengths.shape[1]
    group_len = lengths[0]
    row_ids = exp_index * query_rows + jnp.arange(query_rows, dtype=jnp.int32)
    request, member, position = locate(row_ids, group_len)
    wanted = lax.dynamic_index_in_dim(request_adapter, req_index, 0, keepdims=False)
    slot_ids = jnp.arange(adapter_home_row.shape[0], dtype=jnp.int32)
    home_of = jnp.sum(
        jnp.where(wanted[:, None] == slot_ids[None, :], adapter_home_row[None, :], 0), axis=1
    )
    query_cols = q_local * HEAD_WIDTH
    kv_cols = kv_local * HEAD_WIDTH
    bank_local = query_down_factor.shape[0]
    up_q = lax.dynamic_slice_in_dim(query_up_factor, hid_index * query_cols, query_cols, 2)
    up_v = lax.dynamic_slice_in_dim(value_up_factor, hid_index * kv_cols, kv_cols, 2)
    parts_in = (query_down_factor, up_q, value_down_factor, up_v)
    part_shapes = [p.shape[1:] for p in parts_in]
    part_sizes = [p.shape[1] * p.shape[2] for p in parts_in]
    bank = jnp.concatenate([p.reshape(bank_local, -1) for p in parts_in], axis=1)
    along_req = lax.all_gather(bank, "req", axis=0, tiled=True)
    home_dev = home_of // bank_local
    home_pick = (home_dev // exp_count) * bank_local + home_of % bank_local
    mine = (home_dev % exp_count) == exp_index
    rows_pick = jnp.take(along_req, home_pick, axis=0)
    rows_pick = jnp.where(mine[:, None], rows_pick, jnp.zeros_like(rows_pick))
    rows_all = lax.all_to_all(
        jnp.broadcast_to(rows_pick[None], (exp_count,) + rows_pick.shape),
        "exp",
        split_axis=0,
        concat_axis=0,
        tiled=True,
    )
    rows_pick = rows_all[home_dev % exp_count, jnp.arange(requests, dtype=jnp.int32)]
    chosen = []
    start = 0
    for shape_in, size_in in zip(part_shapes, part_sizes):
        chosen.append(rows_pick[:, start:start + size_in].reshape((requests,) + shape_in))
        start += size_in
    qa_sel, qb_sel, va_sel, vb_sel = chosen
    normed_rows = rms_norm(layer_input_rows, attention_norm_gain)

    def low_rank_term(a_sel, b_sel, width_cols, offset):
        inner_terms = jnp.einsum(
            "td,jdr->tjr", normed_rows, a_sel, preferred_element_type=jnp.float32
        )
        inner_terms = (
            jnp.where(member[:, :, None], inner_terms, 0.0)
            .reshape(query_rows, requests * adapter_rank_size)
            .astype(jnp.bfloat16)
        )
        right_factor = b_sel.reshape(requests * adapter_rank_size, width_cols)
        return jnp.dot(inner_terms, right_factor, preferred_element_type=jnp.float32)

    query_matrix = jnp.dot(
        normed_rows, query_weight, preferred_element_type=jnp.float32
    ) + low_rank_term(qa_sel, qb_sel, query_cols, hid_index * query_cols)
    query_matrix = rotary(query_matrix.reshape(query_rows, q_local, HEAD_WIDTH), position).astype(
        jnp.bfloat16
    )
    query_matrix = query_matrix.reshape(query_rows, kv_local, group_share, HEAD_WIDTH)
    keys_own = jnp.dot(normed_rows, key_weight, preferred_element_type=jnp.float32)
    keys_own = (
        rotary(keys_own.reshape(query_rows, kv_local, HEAD_WIDTH), position)
        .astype(jnp.bfloat16)
        .reshape(query_rows, kv_cols)
    )
    values_own = jnp.dot(
        normed_rows, value_weight, preferred_element_type=jnp.float32
    ) + low_rank_term(va_sel, vb_sel, kv_cols, hid_index * kv_cols)
    values_own = values_own.astype(jnp.bfloat16)
    running_max = jnp.full((kv_local, group_share, query_rows), neg_large, jnp.float32)
    kv_own = jnp.concatenate([keys_own, values_own], axis=1)
    kv_piece = lax.all_to_all(
        jnp.broadcast_to(kv_own[None], (exp_count,) + kv_own.shape),
        "exp",
        split_axis=0,
        concat_axis=0,
        tiled=True,
    ).reshape(exp_count * query_rows, 2 * kv_cols)
    key_piece = kv_piece[:, :kv_cols]
    value_piece = kv_piece[:, kv_cols:]
    piece_len = key_piece.shape[0]
    key_ids = jnp.arange(piece_len, dtype=jnp.int32)
    key_request = request_of(key_ids, group_len)
    allowed = (request[:, None] == key_request[None, :]) & (key_ids[None, :] <= row_ids[:, None])
    key_heads = key_piece.reshape(piece_len, kv_local, HEAD_WIDTH)
    value_heads = value_piece.reshape(piece_len, kv_local, HEAD_WIDTH)
    scores = (
        jnp.einsum("qkgh,nkh->kgqn", query_matrix, key_heads, preferred_element_type=jnp.float32)
        * scale_attn
    )
    scores = jnp.where(allowed[None, None], scores, neg_large)
    new_max = jnp.maximum(running_max, jnp.max(scores, axis=-1))
    weights = jnp.where(allowed[None, None], jnp.exp(scores - new_max[..., None]), 0.0)
    running_sum = jnp.sum(weights, axis=-1)
    running_out = jnp.einsum(
        "kgqn,nkh->kgqh",
        weights.astype(jnp.bfloat16),
        value_heads,
        preferred_element_type=jnp.float32,
    )
    running_max, running_sum, running_out = (new_max, running_sum, running_out)
    attended = (running_out / running_sum[..., None]).astype(jnp.bfloat16)
    attended = jnp.transpose(attended, (2, 0, 1, 3)).reshape(query_rows, query_cols)
    tok_rows = query_rows // hid_count
    head_sums = jnp.dot(attended, attention_output_weight, preferred_element_type=jnp.float32)
    head_sums = head_sums.astype(jnp.bfloat16).reshape(hid_count, tok_rows, width)
    head_sums = lax.all_to_all(head_sums, "hid", split_axis=0, concat_axis=0, tiled=True)
    attn_out = jnp.sum(head_sums.astype(jnp.float32), axis=0).astype(jnp.bfloat16)
    own_rows = lax.dynamic_slice_in_dim(layer_input_rows, hid_index * tok_rows, tok_rows, 0)
    mixed_rows = own_rows.astype(jnp.float32) + residual_mult * attn_out.astype(jnp.float32)
    normed_moe = rms_norm(mixed_rows, expert_norm_gain)
    local_exp = expert_gate_weight.shape[0]
    expert_count = local_exp * exp_count
    top_count = routes.shape[1]
    capacity = max(2, tok_rows // 4)
    flat_route = routes.reshape(tok_rows * top_count)
    route_hits = (flat_route[:, None] == jnp.arange(expert_count, dtype=jnp.int32)[None, :]).astype(
        jnp.int32
    )
    earlier = jnp.cumsum(route_hits, axis=0) - route_hits
    slot_pos = jnp.sum(earlier * route_hits, axis=1)
    slots = slot_pos * expert_count + flat_route
    slot_table = jnp.arange(capacity * expert_count, dtype=jnp.int32)
    placed = jnp.any(
        slot_table[:, None, None] == slots.reshape(tok_rows, top_count)[None], axis=2
    ).astype(jnp.bfloat16)
    outgoing = jnp.dot(placed, normed_moe, preferred_element_type=jnp.float32).astype(jnp.bfloat16)
    outgoing = outgoing.reshape(capacity, expert_count, width)
    partners = exp_count * hid_count
    halves = 2 if capacity % 2 == 0 else 1
    cap_part = capacity // halves
    slot_hit = slots.reshape(tok_rows, top_count)[:, :, None] == slot_table[None, None, :]
    combine = jnp.sum(jnp.where(slot_hit, router_expert_weight[:, :, None], 0.0), axis=1)
    expert_acc = jnp.zeros((tok_rows, width), jnp.float32)
    for half in range(halves):
        part_out = outgoing[half * cap_part:(half + 1) * cap_part]
        copies = jnp.broadcast_to(
            part_out.reshape(cap_part, exp_count, 1, local_exp, width),
            (cap_part, exp_count, hid_count, local_exp, width),
        )
        copies = copies.reshape(cap_part, partners * local_exp, width)
        arrived = lax.all_to_all(copies, ("exp", "hid"), split_axis=1, concat_axis=0, tiled=True)
        partials = expert_rows(
            arrived, expert_gate_weight, expert_up_weight, expert_down_weight
        ).astype(jnp.bfloat16)
        partials = jnp.transpose(
            partials.reshape(partners, cap_part, local_exp, width), (1, 0, 2, 3)
        ).reshape(cap_part, partners * local_exp, width)
        returned = lax.all_to_all(partials, ("exp", "hid"), split_axis=1, concat_axis=1, tiled=True)
        returned = returned.reshape(cap_part, exp_count, hid_count, local_exp, width)
        results = jnp.sum(returned.astype(jnp.float32), axis=2).astype(jnp.bfloat16)
        results = results.reshape(cap_part * expert_count, width)
        part_cols = combine[:, half * cap_part * expert_count:(half + 1) * cap_part * expert_count]
        expert_acc = expert_acc + jnp.dot(
            part_cols,
            results.astype(jnp.float32),
            precision=lax.Precision.HIGHEST,
            preferred_element_type=jnp.float32,
        )
    expert_out = expert_acc.astype(jnp.bfloat16)
    return (attn_out, expert_out)


def solution(mesh):
    in_specs = (
        P(("req", "exp"), None),
        P(),
        P(None, "hid"),
        P(None, "hid"),
        P(None, "hid"),
        P("hid", None),
        P(("req", "exp"), None, None),
        P(("req", "exp"), None, None),
        P(("req", "exp"), None, None),
        P(("req", "exp"), None, None),
        P("req", None),
        P(),
        P(),
        P(),
        P(("req", "exp", "hid"), None),
        P(("req", "exp", "hid"), None),
        P("exp", None, "hid"),
        P("exp", None, "hid"),
        P("exp", "hid", None),
    )
    out_specs = (P(("req", "exp", "hid"), None), P(("req", "exp", "hid"), None))
    return jax.shard_map(
        per_device, mesh=mesh, in_specs=in_specs, out_specs=out_specs, check_vma=False
    )
```

```python
import jax
import jax.numpy as jnp
from jax import lax
from jax.sharding import PartitionSpec as P

HEAD_WIDTH = 64


scale_attn = 0.015625
residual_mult = 0.22
norm_eps = 1e-06
rope_base = 10000.0
neg_large = -1e30


def rms_norm(values, norm_gain):
    widened = values.astype(jnp.float32)
    mean_sq = jnp.mean(widened * widened, axis=-1, keepdims=True)
    return (widened * lax.rsqrt(mean_sq + norm_eps) * norm_gain).astype(jnp.bfloat16)


def rotary(heads_in, position):
    half_size = heads_in.shape[-1] // 2
    frequency = rope_base ** (-2.0 * jnp.arange(half_size, dtype=jnp.float32) / heads_in.shape[-1])
    angles = position.astype(jnp.float32)[:, None] * frequency[None, :]
    cosine = jnp.cos(angles)[:, None, :]
    sine_part = jnp.sin(angles)[:, None, :]
    first_half = heads_in[..., :half_size]
    second_half = heads_in[..., half_size:]
    return jnp.concatenate(
        [
            first_half * cosine - second_half * sine_part,
            second_half * cosine + first_half * sine_part,
        ],
        axis=-1,
    )


def request_of(row_ids, group_len):
    request_end = jnp.cumsum(group_len)
    return jnp.sum((row_ids[:, None] >= request_end[None, :]).astype(jnp.int32), axis=1)


def locate(row_ids, group_len):
    request_end = jnp.cumsum(group_len)
    request_start = request_end - group_len
    request = request_of(row_ids, group_len)
    member = request[:, None] == jnp.arange(group_len.shape[0], dtype=jnp.int32)[None, :]
    position = row_ids - jnp.sum(jnp.where(member, request_start[None, :], 0), axis=1)
    return (request, member, position)


def expert_rows(rows_in, expert_gate_weight, expert_up_weight, expert_down_weight):
    gate_act = jnp.einsum(
        "red,edf->ref", rows_in, expert_gate_weight, preferred_element_type=jnp.float32
    )
    upper = jnp.einsum(
        "red,edf->ref", rows_in, expert_up_weight, preferred_element_type=jnp.float32
    )
    hidden = (jax.nn.silu(gate_act) * upper).astype(jnp.bfloat16)
    return jnp.einsum(
        "ref,efd->red", hidden, expert_down_weight, preferred_element_type=jnp.float32
    )


def per_device(
    layer_input_rows,
    attention_norm_gain,
    query_weight,
    key_weight,
    value_weight,
    attention_output_weight,
    query_down_factor,
    query_up_factor,
    value_down_factor,
    value_up_factor,
    lengths,
    request_adapter,
    adapter_home_row,
    expert_norm_gain,
    routes,
    router_expert_weight,
    expert_gate_weight,
    expert_up_weight,
    expert_down_weight,
):
    exp_count = lax.axis_size("exp")
    hid_count = lax.axis_size("hid")
    exp_index = lax.axis_index("exp")
    hid_index = lax.axis_index("hid")
    req_index = lax.axis_index("req")
    query_rows = layer_input_rows.shape[0]
    width = layer_input_rows.shape[1]
    kv_local = key_weight.shape[1] // HEAD_WIDTH
    q_local = query_weight.shape[1] // HEAD_WIDTH
    group_share = q_local // kv_local
    adapter_rank_size = query_down_factor.shape[2]
    requests = lengths.shape[1]
    group_len = lengths[0]
    row_ids = exp_index * query_rows + jnp.arange(query_rows, dtype=jnp.int32)
    request, member, position = locate(row_ids, group_len)
    wanted = lax.dynamic_index_in_dim(request_adapter, req_index, 0, keepdims=False)
    slot_ids = jnp.arange(adapter_home_row.shape[0], dtype=jnp.int32)
    home_of = jnp.sum(
        jnp.where(wanted[:, None] == slot_ids[None, :], adapter_home_row[None, :], 0), axis=1
    )
    query_cols = q_local * HEAD_WIDTH
    kv_cols = kv_local * HEAD_WIDTH
    bank_local = query_down_factor.shape[0]
    up_q = lax.dynamic_slice_in_dim(query_up_factor, hid_index * query_cols, query_cols, 2)
    up_v = lax.dynamic_slice_in_dim(value_up_factor, hid_index * kv_cols, kv_cols, 2)
    parts_in = (query_down_factor, up_q, value_down_factor, up_v)
    part_shapes = [p.shape[1:] for p in parts_in]
    part_sizes = [p.shape[1] * p.shape[2] for p in parts_in]
    bank = jnp.concatenate([p.reshape(bank_local, -1) for p in parts_in], axis=1)
    req_count = lax.axis_size("req")
    along_req = lax.all_to_all(
        jnp.broadcast_to(bank[None], (req_count,) + bank.shape),
        "req",
        split_axis=0,
        concat_axis=0,
        tiled=True,
    ).reshape(req_count * bank_local, bank.shape[1])
    home_dev = home_of // bank_local
    home_pick = (home_dev // exp_count) * bank_local + home_of % bank_local
    mine = (home_dev % exp_count) == exp_index
    rows_pick = jnp.take(along_req, home_pick, axis=0)
    rows_pick = jnp.where(mine[:, None], rows_pick, jnp.zeros_like(rows_pick))
    rows_all = lax.all_to_all(
        jnp.broadcast_to(rows_pick[None], (exp_count,) + rows_pick.shape),
        "exp",
        split_axis=0,
        concat_axis=0,
        tiled=True,
    )
    rows_pick = rows_all[home_dev % exp_count, jnp.arange(requests, dtype=jnp.int32)]
    chosen = []
    start = 0
    for shape_in, size_in in zip(part_shapes, part_sizes):
        chosen.append(rows_pick[:, start:start + size_in].reshape((requests,) + shape_in))
        start += size_in
    qa_sel, qb_sel, va_sel, vb_sel = chosen
    normed_rows = rms_norm(layer_input_rows, attention_norm_gain)

    def low_rank_term(a_sel, b_sel, width_cols, offset):
        inner_terms = jnp.einsum(
            "td,jdr->tjr", normed_rows, a_sel, preferred_element_type=jnp.float32
        )
        inner_terms = (
            jnp.where(member[:, :, None], inner_terms, 0.0)
            .reshape(query_rows, requests * adapter_rank_size)
            .astype(jnp.bfloat16)
        )
        right_factor = b_sel.reshape(requests * adapter_rank_size, width_cols)
        return jnp.dot(inner_terms, right_factor, preferred_element_type=jnp.float32)

    query_matrix = jnp.dot(
        normed_rows, query_weight, preferred_element_type=jnp.float32
    ) + low_rank_term(qa_sel, qb_sel, query_cols, hid_index * query_cols)
    query_matrix = rotary(query_matrix.reshape(query_rows, q_local, HEAD_WIDTH), position).astype(
        jnp.bfloat16
    )
    query_matrix = query_matrix.reshape(query_rows, kv_local, group_share, HEAD_WIDTH)
    keys_own = jnp.dot(normed_rows, key_weight, preferred_element_type=jnp.float32)
    keys_own = (
        rotary(keys_own.reshape(query_rows, kv_local, HEAD_WIDTH), position)
        .astype(jnp.bfloat16)
        .reshape(query_rows, kv_cols)
    )
    values_own = jnp.dot(
        normed_rows, value_weight, preferred_element_type=jnp.float32
    ) + low_rank_term(va_sel, vb_sel, kv_cols, hid_index * kv_cols)
    values_own = values_own.astype(jnp.bfloat16)
    running_max = jnp.full((kv_local, group_share, query_rows), neg_large, jnp.float32)
    kv_own = jnp.concatenate([keys_own, values_own], axis=1)
    kv_piece = lax.all_to_all(
        jnp.broadcast_to(kv_own[None], (exp_count,) + kv_own.shape),
        "exp",
        split_axis=0,
        concat_axis=0,
        tiled=True,
    ).reshape(exp_count * query_rows, 2 * kv_cols)
    key_piece = kv_piece[:, :kv_cols]
    value_piece = kv_piece[:, kv_cols:]
    piece_len = key_piece.shape[0]
    key_ids = jnp.arange(piece_len, dtype=jnp.int32)
    key_request = request_of(key_ids, group_len)
    allowed = (request[:, None] == key_request[None, :]) & (key_ids[None, :] <= row_ids[:, None])
    key_heads = key_piece.reshape(piece_len, kv_local, HEAD_WIDTH)
    value_heads = value_piece.reshape(piece_len, kv_local, HEAD_WIDTH)
    scores = (
        jnp.einsum("qkgh,nkh->kgqn", query_matrix, key_heads, preferred_element_type=jnp.float32)
        * scale_attn
    )
    scores = jnp.where(allowed[None, None], scores, neg_large)
    new_max = jnp.maximum(running_max, jnp.max(scores, axis=-1))
    weights = jnp.where(allowed[None, None], jnp.exp(scores - new_max[..., None]), 0.0)
    running_sum = jnp.sum(weights, axis=-1)
    running_out = jnp.einsum(
        "kgqn,nkh->kgqh",
        weights.astype(jnp.bfloat16),
        value_heads,
        preferred_element_type=jnp.float32,
    )
    running_max, running_sum, running_out = (new_max, running_sum, running_out)
    attended = (running_out / running_sum[..., None]).astype(jnp.bfloat16)
    attended = jnp.transpose(attended, (2, 0, 1, 3)).reshape(query_rows, query_cols)
    tok_rows = query_rows // hid_count
    head_sums = jnp.dot(attended, attention_output_weight, preferred_element_type=jnp.float32)
    head_sums = head_sums.astype(jnp.bfloat16).reshape(hid_count, tok_rows, width)
    head_sums = lax.all_to_all(head_sums, "hid", split_axis=0, concat_axis=0, tiled=True)
    attn_out = jnp.sum(head_sums.astype(jnp.float32), axis=0).astype(jnp.bfloat16)
    own_rows = lax.dynamic_slice_in_dim(layer_input_rows, hid_index * tok_rows, tok_rows, 0)
    mixed_rows = own_rows.astype(jnp.float32) + residual_mult * attn_out.astype(jnp.float32)
    normed_moe = rms_norm(mixed_rows, expert_norm_gain)
    local_exp = expert_gate_weight.shape[0]
    expert_count = local_exp * exp_count
    top_count = routes.shape[1]
    capacity = max(2, tok_rows // 4)
    flat_route = routes.reshape(tok_rows * top_count)
    route_hits = (flat_route[:, None] == jnp.arange(expert_count, dtype=jnp.int32)[None, :]).astype(
        jnp.int32
    )
    earlier = jnp.cumsum(route_hits, axis=0) - route_hits
    slot_pos = jnp.sum(earlier * route_hits, axis=1)
    slots = slot_pos * expert_count + flat_route
    slot_table = jnp.arange(capacity * expert_count, dtype=jnp.int32)
    placed = jnp.any(
        slot_table[:, None, None] == slots.reshape(tok_rows, top_count)[None], axis=2
    ).astype(jnp.bfloat16)
    outgoing = jnp.dot(placed, normed_moe, preferred_element_type=jnp.float32).astype(jnp.bfloat16)
    outgoing = outgoing.reshape(capacity, expert_count, width)
    partners = exp_count * hid_count
    halves = 2 if capacity % 2 == 0 else 1
    cap_part = capacity // halves
    slot_hit = slots.reshape(tok_rows, top_count)[:, :, None] == slot_table[None, None, :]
    combine = jnp.sum(jnp.where(slot_hit, router_expert_weight[:, :, None], 0.0), axis=1)
    expert_acc = jnp.zeros((tok_rows, width), jnp.float32)
    for half in range(halves):
        part_out = outgoing[half * cap_part:(half + 1) * cap_part]
        copies = jnp.broadcast_to(
            part_out.reshape(cap_part, exp_count, 1, local_exp, width),
            (cap_part, exp_count, hid_count, local_exp, width),
        )
        copies = copies.reshape(cap_part, partners * local_exp, width)
        arrived = lax.all_to_all(copies, ("exp", "hid"), split_axis=1, concat_axis=0, tiled=True)
        partials = expert_rows(
            arrived, expert_gate_weight, expert_up_weight, expert_down_weight
        ).astype(jnp.bfloat16)
        partials = jnp.transpose(
            partials.reshape(partners, cap_part, local_exp, width), (1, 0, 2, 3)
        ).reshape(cap_part, partners * local_exp, width)
        returned = lax.all_to_all(partials, ("exp", "hid"), split_axis=1, concat_axis=1, tiled=True)
        returned = returned.reshape(cap_part, exp_count, hid_count, local_exp, width)
        results = jnp.sum(returned.astype(jnp.float32), axis=2).astype(jnp.bfloat16)
        results = results.reshape(cap_part * expert_count, width)
        part_cols = combine[:, half * cap_part * expert_count:(half + 1) * cap_part * expert_count]
        expert_acc = expert_acc + jnp.dot(
            part_cols,
            results.astype(jnp.float32),
            precision=lax.Precision.HIGHEST,
            preferred_element_type=jnp.float32,
        )
    expert_out = expert_acc.astype(jnp.bfloat16)
    return (attn_out, expert_out)


def solution(mesh):
    in_specs = (
        P(("req", "exp"), None),
        P(),
        P(None, "hid"),
        P(None, "hid"),
        P(None, "hid"),
        P("hid", None),
        P(("req", "exp"), None, None),
        P(("req", "exp"), None, None),
        P(("req", "exp"), None, None),
        P(("req", "exp"), None, None),
        P("req", None),
        P(),
        P(),
        P(),
        P(("req", "exp", "hid"), None),
        P(("req", "exp", "hid"), None),
        P("exp", None, "hid"),
        P("exp", None, "hid"),
        P("exp", "hid", None),
    )
    out_specs = (P(("req", "exp", "hid"), None), P(("req", "exp", "hid"), None))
    return jax.shard_map(
        per_device, mesh=mesh, in_specs=in_specs, out_specs=out_specs, check_vma=False
    )
```

```python
import jax
import jax.numpy as jnp
from jax import lax
from jax.sharding import PartitionSpec as P

HEAD_WIDTH = 64


scale_attn = 0.015625
residual_mult = 0.22
norm_eps = 1e-06
rope_base = 10000.0
neg_large = -1e30


def rms_norm(values, norm_gain):
    widened = values.astype(jnp.float32)
    mean_sq = jnp.mean(widened * widened, axis=-1, keepdims=True)
    return (widened * lax.rsqrt(mean_sq + norm_eps) * norm_gain).astype(jnp.bfloat16)


def rotary(heads_in, position):
    half_size = heads_in.shape[-1] // 2
    frequency = rope_base ** (-2.0 * jnp.arange(half_size, dtype=jnp.float32) / heads_in.shape[-1])
    angles = position.astype(jnp.float32)[:, None] * frequency[None, :]
    cosine = jnp.cos(angles)[:, None, :]
    sine_part = jnp.sin(angles)[:, None, :]
    first_half = heads_in[..., :half_size]
    second_half = heads_in[..., half_size:]
    return jnp.concatenate(
        [
            first_half * cosine - second_half * sine_part,
            second_half * cosine + first_half * sine_part,
        ],
        axis=-1,
    )


def request_of(row_ids, group_len):
    request_end = jnp.cumsum(group_len)
    return jnp.sum((row_ids[:, None] >= request_end[None, :]).astype(jnp.int32), axis=1)


def locate(row_ids, group_len):
    request_end = jnp.cumsum(group_len)
    request_start = request_end - group_len
    request = request_of(row_ids, group_len)
    member = request[:, None] == jnp.arange(group_len.shape[0], dtype=jnp.int32)[None, :]
    position = row_ids - jnp.sum(jnp.where(member, request_start[None, :], 0), axis=1)
    return (request, member, position)


def expert_rows(rows_in, expert_gate_weight, expert_up_weight, expert_down_weight):
    gate_act = jnp.einsum(
        "red,edf->ref", rows_in, expert_gate_weight, preferred_element_type=jnp.float32
    )
    upper = jnp.einsum(
        "red,edf->ref", rows_in, expert_up_weight, preferred_element_type=jnp.float32
    )
    hidden = (jax.nn.silu(gate_act) * upper).astype(jnp.bfloat16)
    return jnp.einsum(
        "ref,efd->red", hidden, expert_down_weight, preferred_element_type=jnp.float32
    )


def per_device(
    layer_input_rows,
    attention_norm_gain,
    query_weight,
    key_weight,
    value_weight,
    attention_output_weight,
    query_down_factor,
    query_up_factor,
    value_down_factor,
    value_up_factor,
    lengths,
    request_adapter,
    adapter_home_row,
    expert_norm_gain,
    routes,
    router_expert_weight,
    expert_gate_weight,
    expert_up_weight,
    expert_down_weight,
):
    exp_count = lax.axis_size("exp")
    hid_count = lax.axis_size("hid")
    exp_index = lax.axis_index("exp")
    hid_index = lax.axis_index("hid")
    req_index = lax.axis_index("req")
    query_rows = layer_input_rows.shape[0]
    width = layer_input_rows.shape[1]
    kv_local = key_weight.shape[1] // HEAD_WIDTH
    q_local = query_weight.shape[1] // HEAD_WIDTH
    group_share = q_local // kv_local
    adapter_rank_size = query_down_factor.shape[2]
    requests = lengths.shape[1]
    group_len = lengths[0]
    row_ids = exp_index * query_rows + jnp.arange(query_rows, dtype=jnp.int32)
    request, member, position = locate(row_ids, group_len)
    wanted = lax.dynamic_index_in_dim(request_adapter, req_index, 0, keepdims=False)
    slot_ids = jnp.arange(adapter_home_row.shape[0], dtype=jnp.int32)
    home_of = jnp.sum(
        jnp.where(wanted[:, None] == slot_ids[None, :], adapter_home_row[None, :], 0), axis=1
    )
    query_cols = q_local * HEAD_WIDTH
    kv_cols = kv_local * HEAD_WIDTH
    bank_local = query_down_factor.shape[0]
    up_q = lax.dynamic_slice_in_dim(query_up_factor, hid_index * query_cols, query_cols, 2)
    up_v = lax.dynamic_slice_in_dim(value_up_factor, hid_index * kv_cols, kv_cols, 2)
    parts_in = (query_down_factor, up_q, value_down_factor, up_v)
    part_shapes = [p.shape[1:] for p in parts_in]
    part_sizes = [p.shape[1] * p.shape[2] for p in parts_in]
    bank = jnp.concatenate([p.reshape(bank_local, -1) for p in parts_in], axis=1)
    along_req = lax.all_gather(bank, "req", axis=0, tiled=True)
    home_dev = home_of // bank_local
    home_pick = (home_dev // exp_count) * bank_local + home_of % bank_local
    mine = (home_dev % exp_count) == exp_index
    rows_pick = jnp.take(along_req, home_pick, axis=0)
    rows_pick = jnp.where(mine[:, None], rows_pick, jnp.zeros_like(rows_pick))
    rows_all = lax.all_to_all(
        jnp.broadcast_to(rows_pick[None], (exp_count,) + rows_pick.shape),
        "exp",
        split_axis=0,
        concat_axis=0,
        tiled=True,
    )
    rows_pick = rows_all[home_dev % exp_count, jnp.arange(requests, dtype=jnp.int32)]
    chosen = []
    start = 0
    for shape_in, size_in in zip(part_shapes, part_sizes):
        chosen.append(rows_pick[:, start:start + size_in].reshape((requests,) + shape_in))
        start += size_in
    qa_sel, qb_sel, va_sel, vb_sel = chosen
    normed_rows = rms_norm(layer_input_rows, attention_norm_gain)

    def low_rank_term(a_sel, b_sel, width_cols, offset):
        inner_terms = jnp.einsum(
            "td,jdr->tjr", normed_rows, a_sel, preferred_element_type=jnp.float32
        )
        inner_terms = (
            jnp.where(member[:, :, None], inner_terms, 0.0)
            .reshape(query_rows, requests * adapter_rank_size)
            .astype(jnp.bfloat16)
        )
        right_factor = b_sel.reshape(requests * adapter_rank_size, width_cols)
        return jnp.dot(inner_terms, right_factor, preferred_element_type=jnp.float32)

    query_matrix = jnp.dot(
        normed_rows, query_weight, preferred_element_type=jnp.float32
    ) + low_rank_term(qa_sel, qb_sel, query_cols, hid_index * query_cols)
    query_matrix = rotary(query_matrix.reshape(query_rows, q_local, HEAD_WIDTH), position).astype(
        jnp.bfloat16
    )
    query_matrix = query_matrix.reshape(query_rows, kv_local, group_share, HEAD_WIDTH)
    keys_own = jnp.dot(normed_rows, key_weight, preferred_element_type=jnp.float32)
    keys_own = (
        rotary(keys_own.reshape(query_rows, kv_local, HEAD_WIDTH), position)
        .astype(jnp.bfloat16)
        .reshape(query_rows, kv_cols)
    )
    values_own = jnp.dot(
        normed_rows, value_weight, preferred_element_type=jnp.float32
    ) + low_rank_term(va_sel, vb_sel, kv_cols, hid_index * kv_cols)
    values_own = values_own.astype(jnp.bfloat16)
    running_max = jnp.full((kv_local, group_share, query_rows), neg_large, jnp.float32)
    kv_own = jnp.concatenate([keys_own, values_own], axis=1)
    kv_piece = lax.all_to_all(
        jnp.broadcast_to(kv_own[None], (exp_count,) + kv_own.shape),
        "exp",
        split_axis=0,
        concat_axis=0,
        tiled=True,
    ).reshape(exp_count * query_rows, 2 * kv_cols)
    key_piece = kv_piece[:, :kv_cols]
    value_piece = kv_piece[:, kv_cols:]
    piece_len = key_piece.shape[0]
    key_ids = jnp.arange(piece_len, dtype=jnp.int32)
    key_request = request_of(key_ids, group_len)
    allowed = (request[:, None] == key_request[None, :]) & (key_ids[None, :] <= row_ids[:, None])
    key_heads = key_piece.reshape(piece_len, kv_local, HEAD_WIDTH)
    value_heads = value_piece.reshape(piece_len, kv_local, HEAD_WIDTH)
    scores = (
        jnp.einsum("qkgh,nkh->kgqn", query_matrix, key_heads, preferred_element_type=jnp.float32)
        * scale_attn
    )
    scores = jnp.where(allowed[None, None], scores, neg_large)
    new_max = jnp.maximum(running_max, jnp.max(scores, axis=-1))
    weights = jnp.where(allowed[None, None], jnp.exp(scores - new_max[..., None]), 0.0)
    running_sum = jnp.sum(weights, axis=-1)
    running_out = jnp.einsum(
        "kgqn,nkh->kgqh",
        weights.astype(jnp.bfloat16),
        value_heads,
        preferred_element_type=jnp.float32,
    )
    running_max, running_sum, running_out = (new_max, running_sum, running_out)
    attended = (running_out / running_sum[..., None]).astype(jnp.bfloat16)
    attended = jnp.transpose(attended, (2, 0, 1, 3)).reshape(query_rows, query_cols)
    tok_rows = query_rows // hid_count
    head_sums = jnp.dot(attended, attention_output_weight, preferred_element_type=jnp.float32)
    head_sums = head_sums.astype(jnp.bfloat16).reshape(hid_count, tok_rows, width)
    head_sums = lax.all_to_all(head_sums, "hid", split_axis=0, concat_axis=0, tiled=True)
    attn_out = jnp.sum(head_sums.astype(jnp.float32), axis=0).astype(jnp.bfloat16)
    own_rows = lax.dynamic_slice_in_dim(layer_input_rows, hid_index * tok_rows, tok_rows, 0)
    mixed_rows = own_rows.astype(jnp.float32) + residual_mult * attn_out.astype(jnp.float32)
    normed_moe = rms_norm(mixed_rows, expert_norm_gain)
    local_exp = expert_gate_weight.shape[0]
    expert_count = local_exp * exp_count
    top_count = routes.shape[1]
    capacity = max(2, tok_rows // 4)
    flat_route = routes.reshape(tok_rows * top_count)
    route_hits = (flat_route[:, None] == jnp.arange(expert_count, dtype=jnp.int32)[None, :]).astype(
        jnp.int32
    )
    earlier = jnp.cumsum(route_hits, axis=0) - route_hits
    slot_pos = jnp.sum(earlier * route_hits, axis=1)
    slots = slot_pos * expert_count + flat_route
    slot_table = jnp.arange(capacity * expert_count, dtype=jnp.int32)
    placed = jnp.any(
        slot_table[:, None, None] == slots.reshape(tok_rows, top_count)[None], axis=2
    ).astype(jnp.bfloat16)
    outgoing = jnp.dot(placed, normed_moe, preferred_element_type=jnp.float32).astype(jnp.bfloat16)
    outgoing = outgoing.reshape(capacity, expert_count, width)
    partners = exp_count * hid_count
    halves = 4 if capacity % 4 == 0 else 1
    cap_part = capacity // halves
    slot_hit = slots.reshape(tok_rows, top_count)[:, :, None] == slot_table[None, None, :]
    combine = jnp.sum(jnp.where(slot_hit, router_expert_weight[:, :, None], 0.0), axis=1)
    expert_acc = jnp.zeros((tok_rows, width), jnp.float32)
    for half in range(halves):
        part_out = outgoing[half * cap_part:(half + 1) * cap_part]
        copies = jnp.broadcast_to(
            part_out.reshape(cap_part, exp_count, 1, local_exp, width),
            (cap_part, exp_count, hid_count, local_exp, width),
        )
        copies = copies.reshape(cap_part, partners * local_exp, width)
        arrived = lax.all_to_all(copies, ("exp", "hid"), split_axis=1, concat_axis=0, tiled=True)
        partials = expert_rows(
            arrived, expert_gate_weight, expert_up_weight, expert_down_weight
        ).astype(jnp.bfloat16)
        partials = jnp.transpose(
            partials.reshape(partners, cap_part, local_exp, width), (1, 0, 2, 3)
        ).reshape(cap_part, partners * local_exp, width)
        returned = lax.all_to_all(partials, ("exp", "hid"), split_axis=1, concat_axis=1, tiled=True)
        returned = returned.reshape(cap_part, exp_count, hid_count, local_exp, width)
        results = jnp.sum(returned.astype(jnp.float32), axis=2).astype(jnp.bfloat16)
        results = results.reshape(cap_part * expert_count, width)
        part_cols = combine[:, half * cap_part * expert_count:(half + 1) * cap_part * expert_count]
        expert_acc = expert_acc + jnp.dot(
            part_cols,
            results.astype(jnp.float32),
            precision=lax.Precision.HIGHEST,
            preferred_element_type=jnp.float32,
        )
    expert_out = expert_acc.astype(jnp.bfloat16)
    return (attn_out, expert_out)


def solution(mesh):
    in_specs = (
        P(("req", "exp"), None),
        P(),
        P(None, "hid"),
        P(None, "hid"),
        P(None, "hid"),
        P("hid", None),
        P(("req", "exp"), None, None),
        P(("req", "exp"), None, None),
        P(("req", "exp"), None, None),
        P(("req", "exp"), None, None),
        P("req", None),
        P(),
        P(),
        P(),
        P(("req", "exp", "hid"), None),
        P(("req", "exp", "hid"), None),
        P("exp", None, "hid"),
        P("exp", None, "hid"),
        P("exp", "hid", None),
    )
    out_specs = (P(("req", "exp", "hid"), None), P(("req", "exp", "hid"), None))
    return jax.shard_map(
        per_device, mesh=mesh, in_specs=in_specs, out_specs=out_specs, check_vma=False
    )
```

```python
import jax
import jax.numpy as jnp
from jax import lax
from jax.sharding import PartitionSpec as P

HEAD_WIDTH = 64


scale_attn = 0.015625
residual_mult = 0.22
norm_eps = 1e-06
rope_base = 10000.0
neg_large = -1e30


def rms_norm(values, norm_gain):
    widened = values.astype(jnp.float32)
    mean_sq = jnp.mean(widened * widened, axis=-1, keepdims=True)
    return (widened * lax.rsqrt(mean_sq + norm_eps) * norm_gain).astype(jnp.bfloat16)


def rotary(heads_in, position):
    half_size = heads_in.shape[-1] // 2
    frequency = rope_base ** (-2.0 * jnp.arange(half_size, dtype=jnp.float32) / heads_in.shape[-1])
    angles = position.astype(jnp.float32)[:, None] * frequency[None, :]
    cosine = jnp.cos(angles)[:, None, :]
    sine_part = jnp.sin(angles)[:, None, :]
    first_half = heads_in[..., :half_size]
    second_half = heads_in[..., half_size:]
    return jnp.concatenate(
        [
            first_half * cosine - second_half * sine_part,
            second_half * cosine + first_half * sine_part,
        ],
        axis=-1,
    )


def request_of(row_ids, group_len):
    request_end = jnp.cumsum(group_len)
    return jnp.sum((row_ids[:, None] >= request_end[None, :]).astype(jnp.int32), axis=1)


def locate(row_ids, group_len):
    request_end = jnp.cumsum(group_len)
    request_start = request_end - group_len
    request = request_of(row_ids, group_len)
    member = request[:, None] == jnp.arange(group_len.shape[0], dtype=jnp.int32)[None, :]
    position = row_ids - jnp.sum(jnp.where(member, request_start[None, :], 0), axis=1)
    return (request, member, position)


def expert_rows(rows_in, expert_gate_weight, expert_up_weight, expert_down_weight):
    gate_act = jnp.einsum(
        "red,edf->ref", rows_in, expert_gate_weight, preferred_element_type=jnp.float32
    )
    upper = jnp.einsum(
        "red,edf->ref", rows_in, expert_up_weight, preferred_element_type=jnp.float32
    )
    hidden = (jax.nn.silu(gate_act) * upper).astype(jnp.bfloat16)
    return jnp.einsum(
        "ref,efd->red", hidden, expert_down_weight, preferred_element_type=jnp.float32
    )


def per_device(
    layer_input_rows,
    attention_norm_gain,
    query_weight,
    key_weight,
    value_weight,
    attention_output_weight,
    query_down_factor,
    query_up_factor,
    value_down_factor,
    value_up_factor,
    lengths,
    request_adapter,
    adapter_home_row,
    expert_norm_gain,
    routes,
    router_expert_weight,
    expert_gate_weight,
    expert_up_weight,
    expert_down_weight,
):
    exp_count = lax.axis_size("exp")
    hid_count = lax.axis_size("hid")
    exp_index = lax.axis_index("exp")
    hid_index = lax.axis_index("hid")
    req_index = lax.axis_index("req")
    query_rows = layer_input_rows.shape[0]
    width = layer_input_rows.shape[1]
    kv_local = key_weight.shape[1] // HEAD_WIDTH
    q_local = query_weight.shape[1] // HEAD_WIDTH
    group_share = q_local // kv_local
    adapter_rank_size = query_down_factor.shape[2]
    requests = lengths.shape[1]
    group_len = lengths[0]
    row_ids = exp_index * query_rows + jnp.arange(query_rows, dtype=jnp.int32)
    request, member, position = locate(row_ids, group_len)
    wanted = lax.dynamic_index_in_dim(request_adapter, req_index, 0, keepdims=False)
    slot_ids = jnp.arange(adapter_home_row.shape[0], dtype=jnp.int32)
    home_of = jnp.sum(
        jnp.where(wanted[:, None] == slot_ids[None, :], adapter_home_row[None, :], 0), axis=1
    )
    query_cols = q_local * HEAD_WIDTH
    kv_cols = kv_local * HEAD_WIDTH
    bank_local = query_down_factor.shape[0]
    up_q = lax.dynamic_slice_in_dim(query_up_factor, hid_index * query_cols, query_cols, 2)
    up_v = lax.dynamic_slice_in_dim(value_up_factor, hid_index * kv_cols, kv_cols, 2)
    parts_in = (query_down_factor, up_q, value_down_factor, up_v)
    part_shapes = [p.shape[1:] for p in parts_in]
    part_sizes = [p.shape[1] * p.shape[2] for p in parts_in]
    bank = jnp.concatenate([p.reshape(bank_local, -1) for p in parts_in], axis=1)
    along_req = lax.all_gather(bank, "req", axis=0, tiled=True)
    home_dev = home_of // bank_local
    home_pick = (home_dev // exp_count) * bank_local + home_of % bank_local
    mine = (home_dev % exp_count) == exp_index
    rows_pick = jnp.take(along_req, home_pick, axis=0)
    rows_pick = jnp.where(mine[:, None], rows_pick, jnp.zeros_like(rows_pick))
    rows_all = lax.all_to_all(
        jnp.broadcast_to(rows_pick[None], (exp_count,) + rows_pick.shape),
        "exp",
        split_axis=0,
        concat_axis=0,
        tiled=True,
    )
    rows_pick = rows_all[home_dev % exp_count, jnp.arange(requests, dtype=jnp.int32)]
    chosen = []
    start = 0
    for shape_in, size_in in zip(part_shapes, part_sizes):
        chosen.append(rows_pick[:, start:start + size_in].reshape((requests,) + shape_in))
        start += size_in
    qa_sel, qb_sel, va_sel, vb_sel = chosen
    normed_rows = rms_norm(layer_input_rows, attention_norm_gain)

    def low_rank_term(a_sel, b_sel, width_cols, offset):
        inner_terms = jnp.einsum(
            "td,jdr->tjr", normed_rows, a_sel, preferred_element_type=jnp.float32
        )
        inner_terms = (
            jnp.where(member[:, :, None], inner_terms, 0.0)
            .reshape(query_rows, requests * adapter_rank_size)
            .astype(jnp.bfloat16)
        )
        right_factor = b_sel.reshape(requests * adapter_rank_size, width_cols)
        return jnp.dot(inner_terms, right_factor, preferred_element_type=jnp.float32)

    query_matrix = jnp.dot(
        normed_rows, query_weight, preferred_element_type=jnp.float32
    ) + low_rank_term(qa_sel, qb_sel, query_cols, hid_index * query_cols)
    query_matrix = rotary(query_matrix.reshape(query_rows, q_local, HEAD_WIDTH), position).astype(
        jnp.bfloat16
    )
    query_matrix = query_matrix.reshape(query_rows, kv_local, group_share, HEAD_WIDTH)
    keys_own = jnp.dot(normed_rows, key_weight, preferred_element_type=jnp.float32)
    keys_own = (
        rotary(keys_own.reshape(query_rows, kv_local, HEAD_WIDTH), position)
        .astype(jnp.bfloat16)
        .reshape(query_rows, kv_cols)
    )
    values_own = jnp.dot(
        normed_rows, value_weight, preferred_element_type=jnp.float32
    ) + low_rank_term(va_sel, vb_sel, kv_cols, hid_index * kv_cols)
    values_own = values_own.astype(jnp.bfloat16)
    running_max = jnp.full((kv_local, group_share, query_rows), neg_large, jnp.float32)
    def exchange(own):
        return lax.all_to_all(
            jnp.broadcast_to(own[None], (exp_count,) + own.shape),
            "exp",
            split_axis=0,
            concat_axis=0,
            tiled=True,
        ).reshape(exp_count * query_rows, own.shape[1])

    key_piece = exchange(keys_own)
    value_piece = exchange(values_own)
    piece_len = key_piece.shape[0]
    key_ids = jnp.arange(piece_len, dtype=jnp.int32)
    key_request = request_of(key_ids, group_len)
    allowed = (request[:, None] == key_request[None, :]) & (key_ids[None, :] <= row_ids[:, None])
    key_heads = key_piece.reshape(piece_len, kv_local, HEAD_WIDTH)
    value_heads = value_piece.reshape(piece_len, kv_local, HEAD_WIDTH)
    scores = (
        jnp.einsum("qkgh,nkh->kgqn", query_matrix, key_heads, preferred_element_type=jnp.float32)
        * scale_attn
    )
    scores = jnp.where(allowed[None, None], scores, neg_large)
    new_max = jnp.maximum(running_max, jnp.max(scores, axis=-1))
    weights = jnp.where(allowed[None, None], jnp.exp(scores - new_max[..., None]), 0.0)
    running_sum = jnp.sum(weights, axis=-1)
    running_out = jnp.einsum(
        "kgqn,nkh->kgqh",
        weights.astype(jnp.bfloat16),
        value_heads,
        preferred_element_type=jnp.float32,
    )
    running_max, running_sum, running_out = (new_max, running_sum, running_out)
    attended = (running_out / running_sum[..., None]).astype(jnp.bfloat16)
    attended = jnp.transpose(attended, (2, 0, 1, 3)).reshape(query_rows, query_cols)
    tok_rows = query_rows // hid_count
    head_sums = jnp.dot(attended, attention_output_weight, preferred_element_type=jnp.float32)
    head_sums = head_sums.astype(jnp.bfloat16).reshape(hid_count, tok_rows, width)
    head_sums = lax.all_to_all(head_sums, "hid", split_axis=0, concat_axis=0, tiled=True)
    attn_out = jnp.sum(head_sums.astype(jnp.float32), axis=0).astype(jnp.bfloat16)
    own_rows = lax.dynamic_slice_in_dim(layer_input_rows, hid_index * tok_rows, tok_rows, 0)
    mixed_rows = own_rows.astype(jnp.float32) + residual_mult * attn_out.astype(jnp.float32)
    normed_moe = rms_norm(mixed_rows, expert_norm_gain)
    local_exp = expert_gate_weight.shape[0]
    expert_count = local_exp * exp_count
    top_count = routes.shape[1]
    capacity = max(2, tok_rows // 4)
    flat_route = routes.reshape(tok_rows * top_count)
    route_hits = (flat_route[:, None] == jnp.arange(expert_count, dtype=jnp.int32)[None, :]).astype(
        jnp.int32
    )
    earlier = jnp.cumsum(route_hits, axis=0) - route_hits
    slot_pos = jnp.sum(earlier * route_hits, axis=1)
    slots = slot_pos * expert_count + flat_route
    slot_table = jnp.arange(capacity * expert_count, dtype=jnp.int32)
    placed = jnp.any(
        slot_table[:, None, None] == slots.reshape(tok_rows, top_count)[None], axis=2
    ).astype(jnp.bfloat16)
    outgoing = jnp.dot(placed, normed_moe, preferred_element_type=jnp.float32).astype(jnp.bfloat16)
    outgoing = outgoing.reshape(capacity, expert_count, width)
    partners = exp_count * hid_count
    halves = 2 if capacity % 2 == 0 else 1
    cap_part = capacity // halves
    slot_hit = slots.reshape(tok_rows, top_count)[:, :, None] == slot_table[None, None, :]
    combine = jnp.sum(jnp.where(slot_hit, router_expert_weight[:, :, None], 0.0), axis=1)
    expert_acc = jnp.zeros((tok_rows, width), jnp.float32)
    for half in range(halves):
        part_out = outgoing[half * cap_part:(half + 1) * cap_part]
        copies = jnp.broadcast_to(
            part_out.reshape(cap_part, exp_count, 1, local_exp, width),
            (cap_part, exp_count, hid_count, local_exp, width),
        )
        copies = copies.reshape(cap_part, partners * local_exp, width)
        arrived = lax.all_to_all(copies, ("exp", "hid"), split_axis=1, concat_axis=0, tiled=True)
        partials = expert_rows(
            arrived, expert_gate_weight, expert_up_weight, expert_down_weight
        ).astype(jnp.bfloat16)
        partials = jnp.transpose(
            partials.reshape(partners, cap_part, local_exp, width), (1, 0, 2, 3)
        ).reshape(cap_part, partners * local_exp, width)
        returned = lax.all_to_all(partials, ("exp", "hid"), split_axis=1, concat_axis=1, tiled=True)
        returned = returned.reshape(cap_part, exp_count, hid_count, local_exp, width)
        results = jnp.sum(returned.astype(jnp.float32), axis=2).astype(jnp.bfloat16)
        results = results.reshape(cap_part * expert_count, width)
        part_cols = combine[:, half * cap_part * expert_count:(half + 1) * cap_part * expert_count]
        expert_acc = expert_acc + jnp.dot(
            part_cols,
            results.astype(jnp.float32),
            precision=lax.Precision.HIGHEST,
            preferred_element_type=jnp.float32,
        )
    expert_out = expert_acc.astype(jnp.bfloat16)
    return (attn_out, expert_out)


def solution(mesh):
    in_specs = (
        P(("req", "exp"), None),
        P(),
        P(None, "hid"),
        P(None, "hid"),
        P(None, "hid"),
        P("hid", None),
        P(("req", "exp"), None, None),
        P(("req", "exp"), None, None),
        P(("req", "exp"), None, None),
        P(("req", "exp"), None, None),
        P("req", None),
        P(),
        P(),
        P(),
        P(("req", "exp", "hid"), None),
        P(("req", "exp", "hid"), None),
        P("exp", None, "hid"),
        P("exp", None, "hid"),
        P("exp", "hid", None),
    )
    out_specs = (P(("req", "exp", "hid"), None), P(("req", "exp", "hid"), None))
    return jax.shard_map(
        per_device, mesh=mesh, in_specs=in_specs, out_specs=out_specs, check_vma=False
    )
```

```python
import jax
import jax.numpy as jnp
from jax import lax
from jax.sharding import PartitionSpec as P

HEAD_WIDTH = 64


scale_attn = 0.015625
residual_mult = 0.22
norm_eps = 1e-06
rope_base = 10000.0
neg_large = -1e30


def rms_norm(values, norm_gain):
    widened = values.astype(jnp.float32)
    mean_sq = jnp.mean(widened * widened, axis=-1, keepdims=True)
    return (widened * lax.rsqrt(mean_sq + norm_eps) * norm_gain).astype(jnp.bfloat16)


def rotary(heads_in, position):
    half_size = heads_in.shape[-1] // 2
    frequency = rope_base ** (-2.0 * jnp.arange(half_size, dtype=jnp.float32) / heads_in.shape[-1])
    angles = position.astype(jnp.float32)[:, None] * frequency[None, :]
    cosine = jnp.cos(angles)[:, None, :]
    sine_part = jnp.sin(angles)[:, None, :]
    first_half = heads_in[..., :half_size]
    second_half = heads_in[..., half_size:]
    return jnp.concatenate(
        [
            first_half * cosine - second_half * sine_part,
            second_half * cosine + first_half * sine_part,
        ],
        axis=-1,
    )


def request_of(row_ids, group_len):
    request_end = jnp.cumsum(group_len)
    return jnp.sum((row_ids[:, None] >= request_end[None, :]).astype(jnp.int32), axis=1)


def locate(row_ids, group_len):
    request_end = jnp.cumsum(group_len)
    request_start = request_end - group_len
    request = request_of(row_ids, group_len)
    member = request[:, None] == jnp.arange(group_len.shape[0], dtype=jnp.int32)[None, :]
    position = row_ids - jnp.sum(jnp.where(member, request_start[None, :], 0), axis=1)
    return (request, member, position)


def expert_rows(rows_in, expert_gate_weight, expert_up_weight, expert_down_weight):
    gate_act = jnp.einsum(
        "red,edf->ref", rows_in, expert_gate_weight, preferred_element_type=jnp.float32
    )
    upper = jnp.einsum(
        "red,edf->ref", rows_in, expert_up_weight, preferred_element_type=jnp.float32
    )
    hidden = (jax.nn.silu(gate_act) * upper).astype(jnp.bfloat16)
    return jnp.einsum(
        "ref,efd->red", hidden, expert_down_weight, preferred_element_type=jnp.float32
    )


def per_device(
    layer_input_rows,
    attention_norm_gain,
    query_weight,
    key_weight,
    value_weight,
    attention_output_weight,
    query_down_factor,
    query_up_factor,
    value_down_factor,
    value_up_factor,
    lengths,
    request_adapter,
    adapter_home_row,
    expert_norm_gain,
    routes,
    router_expert_weight,
    expert_gate_weight,
    expert_up_weight,
    expert_down_weight,
):
    exp_count = lax.axis_size("exp")
    hid_count = lax.axis_size("hid")
    exp_index = lax.axis_index("exp")
    hid_index = lax.axis_index("hid")
    req_index = lax.axis_index("req")
    query_rows = layer_input_rows.shape[0]
    width = layer_input_rows.shape[1]
    kv_local = key_weight.shape[1] // HEAD_WIDTH
    q_local = query_weight.shape[1] // HEAD_WIDTH
    group_share = q_local // kv_local
    adapter_rank_size = query_down_factor.shape[2]
    requests = lengths.shape[1]
    group_len = lengths[0]
    row_ids = exp_index * query_rows + jnp.arange(query_rows, dtype=jnp.int32)
    request, member, position = locate(row_ids, group_len)
    wanted = lax.dynamic_index_in_dim(request_adapter, req_index, 0, keepdims=False)
    slot_ids = jnp.arange(adapter_home_row.shape[0], dtype=jnp.int32)
    home_of = jnp.sum(
        jnp.where(wanted[:, None] == slot_ids[None, :], adapter_home_row[None, :], 0), axis=1
    )
    query_cols = q_local * HEAD_WIDTH
    kv_cols = kv_local * HEAD_WIDTH
    bank_local = query_down_factor.shape[0]
    up_q = lax.dynamic_slice_in_dim(query_up_factor, hid_index * query_cols, query_cols, 2)
    up_v = lax.dynamic_slice_in_dim(value_up_factor, hid_index * kv_cols, kv_cols, 2)
    parts_in = (query_down_factor, up_q, value_down_factor, up_v)
    part_shapes = [p.shape[1:] for p in parts_in]
    part_sizes = [p.shape[1] * p.shape[2] for p in parts_in]
    bank = jnp.concatenate([p.reshape(bank_local, -1) for p in parts_in], axis=1)
    along_req = lax.all_gather(bank, "req", axis=0, tiled=True)
    home_dev = home_of // bank_local
    home_pick = (home_dev // exp_count) * bank_local + home_of % bank_local
    mine = (home_dev % exp_count) == exp_index
    rows_pick = jnp.take(along_req, home_pick, axis=0)
    rows_pick = jnp.where(mine[:, None], rows_pick, jnp.zeros_like(rows_pick))
    rows_all = lax.all_to_all(
        jnp.broadcast_to(rows_pick[None], (exp_count,) + rows_pick.shape),
        "exp",
        split_axis=0,
        concat_axis=0,
        tiled=True,
    )
    rows_pick = rows_all[home_dev % exp_count, jnp.arange(requests, dtype=jnp.int32)]
    chosen = []
    start = 0
    for shape_in, size_in in zip(part_shapes, part_sizes):
        chosen.append(rows_pick[:, start:start + size_in].reshape((requests,) + shape_in))
        start += size_in
    qa_sel, qb_sel, va_sel, vb_sel = chosen
    normed_rows = rms_norm(layer_input_rows, attention_norm_gain)

    def low_rank_term(a_sel, b_sel, width_cols, offset):
        inner_terms = jnp.einsum(
            "td,jdr->tjr", normed_rows, a_sel, preferred_element_type=jnp.float32
        )
        inner_terms = (
            jnp.where(member[:, :, None], inner_terms, 0.0)
            .reshape(query_rows, requests * adapter_rank_size)
            .astype(jnp.bfloat16)
        )
        right_factor = b_sel.reshape(requests * adapter_rank_size, width_cols)
        return jnp.dot(inner_terms, right_factor, preferred_element_type=jnp.float32)

    query_matrix = jnp.dot(
        normed_rows, query_weight, preferred_element_type=jnp.float32
    ) + low_rank_term(qa_sel, qb_sel, query_cols, hid_index * query_cols)
    query_matrix = rotary(query_matrix.reshape(query_rows, q_local, HEAD_WIDTH), position).astype(
        jnp.bfloat16
    )
    query_matrix = query_matrix.reshape(query_rows, kv_local, group_share, HEAD_WIDTH)
    keys_own = jnp.dot(normed_rows, key_weight, preferred_element_type=jnp.float32)
    keys_own = (
        rotary(keys_own.reshape(query_rows, kv_local, HEAD_WIDTH), position)
        .astype(jnp.bfloat16)
        .reshape(query_rows, kv_cols)
    )
    values_own = jnp.dot(
        normed_rows, value_weight, preferred_element_type=jnp.float32
    ) + low_rank_term(va_sel, vb_sel, kv_cols, hid_index * kv_cols)
    values_own = values_own.astype(jnp.bfloat16)
    running_max = jnp.full((kv_local, group_share, query_rows), neg_large, jnp.float32)
    kv_own = jnp.concatenate([keys_own, values_own], axis=1)
    kv_piece = lax.all_to_all(
        jnp.broadcast_to(kv_own[None], (exp_count,) + kv_own.shape),
        "exp",
        split_axis=0,
        concat_axis=0,
        tiled=True,
    ).reshape(exp_count * query_rows, 2 * kv_cols)
    key_piece = kv_piece[:, :kv_cols]
    value_piece = kv_piece[:, kv_cols:]
    piece_len = key_piece.shape[0]
    key_ids = jnp.arange(piece_len, dtype=jnp.int32)
    key_request = request_of(key_ids, group_len)
    allowed = (request[:, None] == key_request[None, :]) & (key_ids[None, :] <= row_ids[:, None])
    key_heads = key_piece.reshape(piece_len, kv_local, HEAD_WIDTH)
    value_heads = value_piece.reshape(piece_len, kv_local, HEAD_WIDTH)
    scores = (
        jnp.einsum("qkgh,nkh->kgqn", query_matrix, key_heads, preferred_element_type=jnp.float32)
        * scale_attn
    )
    scores = jnp.where(allowed[None, None], scores, neg_large)
    new_max = jnp.maximum(running_max, jnp.max(scores, axis=-1))
    weights = jnp.where(allowed[None, None], jnp.exp(scores - new_max[..., None]), 0.0)
    running_sum = jnp.sum(weights, axis=-1)
    running_out = jnp.einsum(
        "kgqn,nkh->kgqh",
        weights.astype(jnp.bfloat16),
        value_heads,
        preferred_element_type=jnp.float32,
    )
    running_max, running_sum, running_out = (new_max, running_sum, running_out)
    attended = (running_out / running_sum[..., None]).astype(jnp.bfloat16)
    attended = jnp.transpose(attended, (2, 0, 1, 3)).reshape(query_rows, query_cols)
    tok_rows = query_rows // hid_count
    head_sums = jnp.dot(attended, attention_output_weight, preferred_element_type=jnp.float32)
    head_sums = head_sums.astype(jnp.bfloat16).reshape(hid_count, tok_rows, width)
    head_sums = lax.all_to_all(head_sums, "hid", split_axis=0, concat_axis=0, tiled=True)
    attn_out = jnp.sum(head_sums.astype(jnp.float32), axis=0).astype(jnp.bfloat16)
    own_rows = lax.dynamic_slice_in_dim(layer_input_rows, hid_index * tok_rows, tok_rows, 0)
    mixed_rows = own_rows.astype(jnp.float32) + residual_mult * attn_out.astype(jnp.float32)
    normed_moe = rms_norm(mixed_rows, expert_norm_gain)
    local_exp = expert_gate_weight.shape[0]
    expert_count = local_exp * exp_count
    top_count = routes.shape[1]
    capacity = max(2, tok_rows // 4)
    flat_route = routes.reshape(tok_rows * top_count)
    route_hits = (flat_route[:, None] == jnp.arange(expert_count, dtype=jnp.int32)[None, :]).astype(
        jnp.int32
    )
    earlier = jnp.cumsum(route_hits, axis=0) - route_hits
    slot_pos = jnp.sum(earlier * route_hits, axis=1)
    slots = slot_pos * expert_count + flat_route
    slot_table = jnp.arange(capacity * expert_count, dtype=jnp.int32)
    placed = jnp.any(
        slot_table[:, None, None] == slots.reshape(tok_rows, top_count)[None], axis=2
    ).astype(jnp.bfloat16)
    outgoing = jnp.dot(placed, normed_moe, preferred_element_type=jnp.float32).astype(jnp.bfloat16)
    outgoing = outgoing.reshape(capacity, expert_count, width)
    partners = exp_count * hid_count
    first_part = (capacity * 5 + 7) // 8
    bounds = [(0, first_part), (first_part, capacity)] if 0 < first_part < capacity else [(0, capacity)]
    slot_hit = slots.reshape(tok_rows, top_count)[:, :, None] == slot_table[None, None, :]
    combine = jnp.sum(jnp.where(slot_hit, router_expert_weight[:, :, None], 0.0), axis=1)
    expert_acc = jnp.zeros((tok_rows, width), jnp.float32)
    for lo, hi in bounds:
        cap_part = hi - lo
        part_out = outgoing[lo:hi]
        copies = jnp.broadcast_to(
            part_out.reshape(cap_part, exp_count, 1, local_exp, width),
            (cap_part, exp_count, hid_count, local_exp, width),
        )
        copies = copies.reshape(cap_part, partners * local_exp, width)
        arrived = lax.all_to_all(copies, ("exp", "hid"), split_axis=1, concat_axis=0, tiled=True)
        partials = expert_rows(
            arrived, expert_gate_weight, expert_up_weight, expert_down_weight
        ).astype(jnp.bfloat16)
        partials = jnp.transpose(
            partials.reshape(partners, cap_part, local_exp, width), (1, 0, 2, 3)
        ).reshape(cap_part, partners * local_exp, width)
        returned = lax.all_to_all(partials, ("exp", "hid"), split_axis=1, concat_axis=1, tiled=True)
        returned = returned.reshape(cap_part, exp_count, hid_count, local_exp, width)
        results = jnp.sum(returned.astype(jnp.float32), axis=2).astype(jnp.bfloat16)
        results = results.reshape(cap_part * expert_count, width)
        part_cols = combine[:, lo * expert_count:hi * expert_count]
        expert_acc = expert_acc + jnp.dot(
            part_cols,
            results.astype(jnp.float32),
            precision=lax.Precision.HIGHEST,
            preferred_element_type=jnp.float32,
        )
    expert_out = expert_acc.astype(jnp.bfloat16)
    return (attn_out, expert_out)


def solution(mesh):
    in_specs = (
        P(("req", "exp"), None),
        P(),
        P(None, "hid"),
        P(None, "hid"),
        P(None, "hid"),
        P("hid", None),
        P(("req", "exp"), None, None),
        P(("req", "exp"), None, None),
        P(("req", "exp"), None, None),
        P(("req", "exp"), None, None),
        P("req", None),
        P(),
        P(),
        P(),
        P(("req", "exp", "hid"), None),
        P(("req", "exp", "hid"), None),
        P("exp", None, "hid"),
        P("exp", None, "hid"),
        P("exp", "hid", None),
    )
    out_specs = (P(("req", "exp", "hid"), None), P(("req", "exp", "hid"), None))
    return jax.shard_map(
        per_device, mesh=mesh, in_specs=in_specs, out_specs=out_specs, check_vma=False
    )
```
